256 devices in a mesh: link: 64 (over x, z, core), col: 4 (over y).
Axes of the slice: x: 4, y: 4, z: 8, core: 2. Of those that a mesh axis runs over, the one named last changes fastest.
Arguments:
- values: bfloat16 [1024, 16, 128], P('link'), may hold values from -6 to 6
- tiles: int32 [1024, 16], P('link'), may hold values from 0 to 127, all different within a row
- barrier: float32 [1024], P('link'), may hold values from 0.5 to 2
- slack: float32 [16384], replicated, may hold values from 0.5 to 2
- order: int32 [128], replicated, may hold values from 0 to 127, each once
Outputs:
- factored: float32 [16384, 16384], P('link', 'col')
The draws below stay inside these ranges and needn't reach their ends.
Inputs may be any that keep to these rules, and one draw needn't show every extreme that they name: `tiles`: each commodity's 16 tile numbers are distinct, and every tile is named by some commodity. `order`: each tile number appears once.
All inputs are finite; a program needn't handle non-finite values.
Results may differ from the reference program's by a relative error of at most 0.0038.
Values may be sent and summed in bfloat16 or wider, within the bound.
No kernel may reach another device: no remote copies, remote signals or barrier semaphores. Data moves between devices by JAX's collectives and lax.ppermute only.
A program may use at most 64 MiB of HBM per device.

```python
import jax
import jax.numpy as jnp
from jax import lax

TILE = 128
TPC = 16
PANEL = 128
K = 1024
LINKS = 16384
LTILES = 128


def shard_levels(key, shape, split, smallest, largest):
    def one(axis_at, parts):
        draws = jax.random.uniform(jax.random.fold_in(jax.random.fold_in(key, 6), axis_at), (parts,), jnp.float32, smallest / len(split), largest / len(split))
        return jnp.repeat(jnp.exp(draws), shape[axis_at] // parts).reshape((-1,) + (1,) * (len(shape) - axis_at - 1))

    loudness = one(*split[0])
    for cut in split[1:]:
        loudness = loudness * one(*cut)
    return loudness


def different_ones(own_key, rows, number_of, top, lift):
    ranking = jax.random.permutation(jax.random.fold_in(own_key, 1), number_of)
    pull = ranking
    for power in range(3):
        pull = pull * pull // number_of
    pull = pull * lift // number_of
    tickets = jax.random.randint(jax.random.fold_in(own_key, 2), (rows, number_of), 0, 4096) + pull
    fixed_rows = jax.random.permutation(jax.random.fold_in(own_key, 3), rows)[jnp.arange(number_of) % rows]
    tickets = jnp.where(jnp.arange(rows)[:, None] == fixed_rows[None, :], 1 << 14, tickets)
    merit = tickets * number_of + jnp.arange(number_of)
    return lax.top_k(merit.astype(jnp.int32), top)[1].astype(jnp.int32)


def noise(own_key, dims, scale, limit, pieces=(), dtype=jnp.bfloat16):
    result = jax.random.normal(own_key, dims, jnp.float32) * scale
    if len(pieces) > 0:
        result = shard_levels(own_key, dims, pieces, -0.22, 0.18) * result
    return jnp.clip(result, min=-limit, max=limit).astype(dtype)


def setup_inputs(seed: int = 0) -> dict:
    splits = jax.random.split(jax.random.key(seed), 6)
    values = noise(splits[0], (K, TPC, TILE), 1.0, 6.0, ((0, 64),))
    tiles = different_ones(splits[1], K, LTILES, TPC, 0)
    barrier = jnp.clip(0.5 + 1.5 * jax.random.uniform(splits[2], (K,), jnp.float32) ** shard_levels(splits[2], (K,), ((0, 64),), -0.2, 0.2), 0.5, 2.0)
    slack = jnp.clip(jax.random.uniform(splits[3], (LINKS,), jnp.float32, 0.5, 2.0), 0.5, 2.0)
    order = jax.random.permutation(splits[4], LTILES).astype(jnp.int32)
    return {"values": values, "tiles": tiles, "barrier": barrier, "slack": slack, "order": order}


def reference(values, tiles, barrier, slack, order):
    factor = LINKS / (K * TPC * TILE)
    scaled = (jnp.sqrt(barrier * factor)[:, None, None] * values.astype(jnp.float32)).astype(jnp.bfloat16)
    onehot = (tiles[:, :, None] == order[None, None, :]).astype(jnp.float32)
    incidence = jnp.einsum('kjp,kju->kpu', onehot, scaled.astype(jnp.float32)).astype(jnp.bfloat16)
    incidence = incidence.reshape(K, LINKS)
    normal = jnp.dot(incidence.T.astype(jnp.float32), incidence.astype(jnp.float32), preferred_element_type=jnp.float32)
    slack_ord = slack.reshape(LTILES, TILE)[order].reshape(LINKS)
    diag_ids = jnp.arange(LINKS)
    matrix = normal.at[diag_ids, diag_ids].add(slack_ord)
    panels = []
    for panel_no in range(2):
        first_col = panel_no * PANEL
        lower_fac = jnp.linalg.cholesky(matrix[first_col:first_col + PANEL, first_col:first_col + PANEL])
        below_rows = matrix[first_col + PANEL:, first_col:first_col + PANEL]
        solved = jax.scipy.linalg.solve_triangular(lower_fac, below_rows.T, lower=True).T
        column = jnp.concatenate([jnp.zeros((first_col, PANEL), jnp.float32), lower_fac, solved], 0)
        rounded = column.astype(jnp.bfloat16)
        matrix = matrix - jnp.dot(rounded.astype(jnp.float32), rounded.T.astype(jnp.float32), preferred_element_type=jnp.float32)
        panels.append(column)
    rows_all = jnp.arange(LINKS)
    matrix = jnp.where(rows_all[:, None] < 2 * PANEL, jnp.float32(0.0), matrix)
    return matrix.at[:, :2 * PANEL].set(jnp.concatenate(panels, 1))
```

```python
import jax
import jax.numpy as jnp
from jax import lax
from jax.sharding import PartitionSpec as P

PANEL = 128
HI = lax.Precision.HIGHEST


def densify(tile_vals, tile_ids, targets):
    onehot = (tile_ids[:, :, None] == targets[None, None, :]).astype(jnp.bfloat16)
    dense_out = jnp.einsum("kjp,kju->kpu", onehot, tile_vals, preferred_element_type=jnp.float32)
    dense_out = dense_out.astype(jnp.bfloat16)
    return dense_out.reshape(tile_vals.shape[0], targets.shape[0] * tile_vals.shape[2])


def contract_rows(left_side, right_side):
    return lax.dot_general(
        left_side, right_side, (((0,), (0,)), ((), ())), preferred_element_type=jnp.float32
    )


def lower_inverse(lower):
    eye = jnp.eye(lower.shape[0], dtype=jnp.float32)
    return jax.scipy.linalg.solve_triangular(lower, eye, lower=True)


def solve_rows(block, inv_lower):
    return lax.dot_general(
        block, inv_lower, (((1,), (1,)), ((), ())), precision=HI,
        preferred_element_type=jnp.float32,
    )


def head_fix(solved, at_top, head):
    top = jnp.where(at_top, head, solved[: head.shape[0]])
    return jnp.concatenate([top, solved[head.shape[0]:]], 0)


def local(values, tiles, barrier, slack, order):
    link_devs = lax.axis_size("link")
    col_devs = lax.axis_size("col")
    link_idx = lax.axis_index("link")
    col_idx = lax.axis_index("col")
    link_count = slack.shape[0]
    rows_dev = link_count // link_devs
    cols_dev = link_count // col_devs
    per_dev, tpc, tile_len = values.shape
    ntiles = order.shape[0]
    lead = 2 * PANEL
    factor = link_count / (per_dev * link_devs * tpc * tile_len)
    scaled = (jnp.sqrt(barrier * factor)[:, None, None] * values.astype(jnp.float32)).astype(
        jnp.bfloat16
    )
    ids = jnp.pad(tiles.astype(jnp.bfloat16), ((0, 0), (0, tile_len - tpc)))
    packed = jnp.concatenate([scaled.reshape(per_dev, tpc * tile_len), ids], 1)
    everyone = lax.all_gather(packed, "link", axis=0, tiled=True)
    kall = everyone.shape[0]
    vals_all = everyone[:, : tpc * tile_len].reshape(kall, tpc, tile_len)
    ids_all = everyone[:, tpc * tile_len : tpc * tile_len + tpc].astype(jnp.int32)

    row_tiles = rows_dev // tile_len
    col_tiles = cols_dev // tile_len
    lead_tiles = lead // tile_len
    inc_lead = densify(vals_all, ids_all, order[:lead_tiles])
    inc_rows = densify(
        vals_all, ids_all, lax.dynamic_slice_in_dim(order, link_idx * row_tiles, row_tiles)
    )
    inc_cols = densify(
        vals_all, ids_all, lax.dynamic_slice_in_dim(order, col_idx * col_tiles, col_tiles)
    )

    slack_ord = jnp.take(slack.reshape(ntiles, tile_len), order, axis=0).reshape(link_count)
    rows_g = link_idx * rows_dev + jnp.arange(rows_dev)
    cols_g = col_idx * cols_dev + jnp.arange(cols_dev)
    lead_g = jnp.arange(lead)

    def lead_cols(inc_x, x_g, start):
        base = contract_rows(inc_x, inc_lead)
        slack_x = lax.dynamic_slice_in_dim(slack_ord, start, x_g.shape[0])
        diag = jnp.where(x_g[:, None] == lead_g[None, :], slack_x[:, None], 0.0)
        return base + diag

    a_lead = lead_cols(inc_lead, lead_g, 0)
    m_rows = lead_cols(inc_rows, rows_g, link_idx * rows_dev)
    m_cols = lead_cols(inc_cols, cols_g, col_idx * cols_dev)

    f0, f1 = 0, PANEL
    l0 = jnp.linalg.cholesky(a_lead[f0:f1, f0:f1])
    inv0 = lower_inverse(l0)
    b0 = solve_rows(a_lead[f1:, f0:f1], inv0)
    head0 = jnp.concatenate([l0, b0], 0)
    rb0 = b0.astype(jnp.bfloat16)
    a11 = a_lead[f1:, f1:] - lax.dot_general(
        rb0, rb0, (((1,), (1,)), ((), ())), preferred_element_type=jnp.float32
    )
    l1 = jnp.linalg.cholesky(a11)
    inv1 = lower_inverse(l1)
    head1 = jnp.concatenate([jnp.zeros_like(l1), l1], 0)

    def panels(m_x, at_top):
        col0 = head_fix(solve_rows(m_x[:, f0:f1], inv0), at_top, head0)
        r0 = col0.astype(jnp.bfloat16)
        m1 = m_x[:, f1:] - lax.dot_general(
            r0, rb0, (((1,), (1,)), ((), ())), preferred_element_type=jnp.float32
        )
        col1 = head_fix(solve_rows(m1, inv1), at_top, head1)
        return col0, col1

    col0_r, col1_r = panels(m_rows, link_idx == 0)
    col0_c, col1_c = panels(m_cols, col_idx == 0)
    left_t = jnp.concatenate(
        [inc_rows, col0_r.astype(jnp.bfloat16).T, col1_r.astype(jnp.bfloat16).T], 0
    )
    right_t = jnp.concatenate(
        [inc_cols, -col0_c.astype(jnp.bfloat16).T, -col1_c.astype(jnp.bfloat16).T], 0
    )
    matrix = contract_rows(left_t, right_t)
    slack_rows = lax.dynamic_slice_in_dim(slack_ord, link_idx * rows_dev, rows_dev)
    matrix = matrix + jnp.where(
        rows_g[:, None] == cols_g[None, :], slack_rows[:, None], jnp.float32(0.0)
    )
    panel_block = jnp.concatenate([col0_r, col1_r], 1)
    padded = jnp.pad(panel_block, ((0, 0), (0, cols_dev - lead)))
    return jnp.where(
        cols_g[None, :] < lead,
        padded,
        jnp.where(rows_g[:, None] < lead, jnp.float32(0.0), matrix),
    )


def solution(mesh):
    in_specs = (P("link", None, None), P("link", None), P("link"), P(), P())
    out_specs = P("link", "col")
    return jax.shard_map(local, mesh=mesh, in_specs=in_specs, out_specs=out_specs, check_vma=False)
```

```python
import jax
import jax.numpy as jnp
from jax import lax
from jax.sharding import PartitionSpec as P

PANEL = 128
HI = lax.Precision.HIGHEST


SUB = 8


def densify(tile_vals, tile_ids, targets):
    kall, tpc, tile_len = tile_vals.shape
    nt = targets.shape[0]
    blocks = kall // SUB
    hot = (tile_ids[:, :, None] == targets[None, None, :]).reshape(blocks, SUB, tpc, nt)
    eye = jnp.eye(SUB, dtype=jnp.bool_)
    spread = hot[:, None] & eye[None, :, :, None, None]
    spread = spread.transpose(0, 4, 1, 2, 3).reshape(blocks, nt * SUB, SUB * tpc)
    dense_out = lax.dot_general(
        spread.astype(jnp.bfloat16), tile_vals.reshape(blocks, SUB * tpc, tile_len),
        (((2,), (1,)), ((0,), (0,))), preferred_element_type=jnp.float32,
    )
    dense_out = dense_out.astype(jnp.bfloat16).reshape(blocks, nt, SUB, tile_len)
    return dense_out.transpose(0, 2, 1, 3).reshape(kall, nt * tile_len)


def gather_links(part, link_devs):
    cores = 2
    zs = 8
    xs = link_devs // (zs * cores)

    def shifted(block, move):
        pairs = [(src, move(src)) for src in range(link_devs)]
        return lax.ppermute(block, "link", pairs)

    def zmove(step):
        return lambda l: (l // (zs * cores)) * zs * cores + (((l // cores) % zs + step) % zs) * cores + l % cores

    def xmove(step):
        return lambda l: ((l // (zs * cores) + step) % xs) * zs * cores + l % (zs * cores)

    got = jnp.concatenate([part] + [shifted(part, zmove(s)) for s in range(1, zs)], 0)
    got = jnp.concatenate([got] + [shifted(got, xmove(s)) for s in range(1, xs)], 0)
    return jnp.concatenate([got, shifted(got, lambda l: l ^ 1)], 0)


def contract_rows(left_side, right_side):
    return lax.dot_general(
        left_side, right_side, (((0,), (0,)), ((), ())), preferred_element_type=jnp.float32
    )


def lower_inverse(lower):
    eye = jnp.eye(lower.shape[0], dtype=jnp.float32)
    return jax.scipy.linalg.solve_triangular(lower, eye, lower=True)


def solve_rows(block, inv_lower):
    return lax.dot_general(
        block, inv_lower, (((1,), (1,)), ((), ())), precision=HI,
        preferred_element_type=jnp.float32,
    )


def head_fix(solved, at_top, head):
    top = jnp.where(at_top, head, solved[: head.shape[0]])
    return jnp.concatenate([top, solved[head.shape[0]:]], 0)


def local(values, tiles, barrier, slack, order):
    link_devs = lax.axis_size("link")
    col_devs = lax.axis_size("col")
    link_idx = lax.axis_index("link")
    col_idx = lax.axis_index("col")
    link_count = slack.shape[0]
    rows_dev = link_count // link_devs
    cols_dev = link_count // col_devs
    per_dev, tpc, tile_len = values.shape
    ntiles = order.shape[0]
    lead = 2 * PANEL
    factor = link_count / (per_dev * link_devs * tpc * tile_len)
    scaled = (jnp.sqrt(barrier * factor)[:, None, None] * values.astype(jnp.float32)).astype(
        jnp.bfloat16
    )
    ids = jnp.pad(tiles.astype(jnp.bfloat16), ((0, 0), (0, tile_len - tpc)))
    packed = jnp.concatenate([scaled.reshape(per_dev, tpc * tile_len), ids], 1)
    everyone = gather_links(packed, link_devs)
    kall = everyone.shape[0]
    vals_all = everyone[:, : tpc * tile_len].reshape(kall, tpc, tile_len)
    ids_all = everyone[:, tpc * tile_len : tpc * tile_len + tpc].astype(jnp.int32)

    row_tiles = rows_dev // tile_len
    col_tiles = cols_dev // tile_len
    lead_tiles = lead // tile_len
    inc_lead = densify(vals_all, ids_all, order[:lead_tiles])
    inc_rows = densify(
        vals_all, ids_all, lax.dynamic_slice_in_dim(order, link_idx * row_tiles, row_tiles)
    )
    inc_cols = densify(
        vals_all, ids_all, lax.dynamic_slice_in_dim(order, col_idx * col_tiles, col_tiles)
    )

    slack_ord = jnp.take(slack.reshape(ntiles, tile_len), order, axis=0).reshape(link_count)
    rows_g = link_idx * rows_dev + jnp.arange(rows_dev)
    cols_g = col_idx * cols_dev + jnp.arange(cols_dev)
    lead_g = jnp.arange(lead)

    def lead_cols(inc_x, x_g, start):
        base = contract_rows(inc_x, inc_lead)
        slack_x = lax.dynamic_slice_in_dim(slack_ord, start, x_g.shape[0])
        diag = jnp.where(x_g[:, None] == lead_g[None, :], slack_x[:, None], 0.0)
        return base + diag

    a_lead = lead_cols(inc_lead, lead_g, 0)
    m_rows = lead_cols(inc_rows, rows_g, link_idx * rows_dev)
    m_cols = lead_cols(inc_cols, cols_g, col_idx * cols_dev)

    f0, f1 = 0, PANEL
    l0 = jnp.linalg.cholesky(a_lead[f0:f1, f0:f1])
    inv0 = lower_inverse(l0)
    b0 = solve_rows(a_lead[f1:, f0:f1], inv0)
    head0 = jnp.concatenate([l0, b0], 0)
    rb0 = b0.astype(jnp.bfloat16)
    a11 = a_lead[f1:, f1:] - lax.dot_general(
        rb0, rb0, (((1,), (1,)), ((), ())), preferred_element_type=jnp.float32
    )
    l1 = jnp.linalg.cholesky(a11)
    inv1 = lower_inverse(l1)
    head1 = jnp.concatenate([jnp.zeros_like(l1), l1], 0)

    def panels(m_x, at_top):
        col0 = head_fix(solve_rows(m_x[:, f0:f1], inv0), at_top, head0)
        r0 = col0.astype(jnp.bfloat16)
        m1 = m_x[:, f1:] - lax.dot_general(
            r0, rb0, (((1,), (1,)), ((), ())), preferred_element_type=jnp.float32
        )
        col1 = head_fix(solve_rows(m1, inv1), at_top, head1)
        return col0, col1

    col0_r, col1_r = panels(m_rows, link_idx == 0)
    col0_c, col1_c = panels(m_cols, col_idx == 0)
    left_t = jnp.concatenate(
        [inc_rows, col0_r.astype(jnp.bfloat16).T, col1_r.astype(jnp.bfloat16).T], 0
    )
    right_t = jnp.concatenate(
        [inc_cols, -col0_c.astype(jnp.bfloat16).T, -col1_c.astype(jnp.bfloat16).T], 0
    )
    matrix = contract_rows(left_t, right_t)
    slack_rows = lax.dynamic_slice_in_dim(slack_ord, link_idx * rows_dev, rows_dev)
    matrix = matrix + jnp.where(
        rows_g[:, None] == cols_g[None, :], slack_rows[:, None], jnp.float32(0.0)
    )
    panel_block = jnp.concatenate([col0_r, col1_r], 1)
    padded = jnp.pad(panel_block, ((0, 0), (0, cols_dev - lead)))
    return jnp.where(
        cols_g[None, :] < lead,
        padded,
        jnp.where(rows_g[:, None] < lead, jnp.float32(0.0), matrix),
    )


def solution(mesh):
    in_specs = (P("link", None, None), P("link", None), P("link"), P(), P())
    out_specs = P("link", "col")
    return jax.shard_map(local, mesh=mesh, in_specs=in_specs, out_specs=out_specs, check_vma=False)
```

```python
import jax
import jax.numpy as jnp
from jax import lax
from jax.sharding import PartitionSpec as P

PANEL = 128
SUB = 8
HI = lax.Precision.HIGHEST


def densify(blocks, ids_full, targets, per_dev, tpc):
    devs, rows, tile_len = blocks.shape
    nt = targets.shape[0]
    groups = per_dev // SUB
    out_rows = groups * nt * SUB
    row_ids = jnp.arange(out_rows)
    row_target = targets[(row_ids // SUB) % nt]
    row_k = (row_ids // (nt * SUB)) * SUB + row_ids % SUB
    col_k = jnp.arange(rows) // tpc
    spread = (ids_full[:, None, :] == row_target[None, :, None]) & (
        row_k[:, None] == col_k[None, :]
    )[None]
    dense_out = lax.dot_general(
        spread.astype(jnp.bfloat16), blocks,
        (((2,), (1,)), ((0,), (0,))), preferred_element_type=jnp.float32,
    )
    dense_out = dense_out.astype(jnp.bfloat16).reshape(devs, groups, nt, SUB, tile_len)
    return dense_out.transpose(0, 1, 3, 2, 4).reshape(devs * per_dev, nt * tile_len)


def gather_links(part, link_devs):
    cores = 2
    zs = 8
    xs = link_devs // (zs * cores)

    def shifted(block, move):
        pairs = [(src, move(src)) for src in range(link_devs)]
        return lax.ppermute(block, "link", pairs)

    def zmove(step):
        return lambda l: (l // (zs * cores)) * zs * cores + (((l // cores) % zs + step) % zs) * cores + l % cores

    def xmove(step):
        return lambda l: ((l // (zs * cores) + step) % xs) * zs * cores + l % (zs * cores)

    got = jnp.stack([part] + [shifted(part, zmove(s)) for s in range(1, zs)], 0)
    got = jnp.concatenate([got] + [shifted(got, xmove(s)) for s in range(1, xs)], 0)
    return jnp.concatenate([got, shifted(got, lambda l: l ^ 1)], 0)


def contract_rows(left_side, right_side):
    return lax.dot_general(
        left_side, right_side, (((0,), (0,)), ((), ())), preferred_element_type=jnp.float32
    )


def lower_inverse(lower):
    eye = jnp.eye(lower.shape[0], dtype=jnp.float32)
    return jax.scipy.linalg.solve_triangular(lower, eye, lower=True)


def solve_rows(block, inv_lower):
    return lax.dot_general(
        block, inv_lower, (((1,), (1,)), ((), ())), precision=HI,
        preferred_element_type=jnp.float32,
    )


def head_fix(solved, at_top, head):
    top = jnp.where(at_top, head, solved[: head.shape[0]])
    return jnp.concatenate([top, solved[head.shape[0]:]], 0)


def local(values, tiles, barrier, slack, order):
    link_devs = lax.axis_size("link")
    col_devs = lax.axis_size("col")
    link_idx = lax.axis_index("link")
    col_idx = lax.axis_index("col")
    link_count = slack.shape[0]
    rows_dev = link_count // link_devs
    cols_dev = link_count // col_devs
    per_dev, tpc, tile_len = values.shape
    ntiles = order.shape[0]
    lead = 2 * PANEL
    lead_tiles = lead // tile_len
    row_tiles = rows_dev // tile_len
    col_tiles = cols_dev // tile_len
    factor = link_count / (per_dev * link_devs * tpc * tile_len)
    scaled = (jnp.sqrt(barrier * factor)[:, None, None] * values.astype(jnp.float32)).astype(
        jnp.bfloat16
    )
    own_rows = scaled.reshape(per_dev * tpc, tile_len)
    own_ids = jnp.pad(tiles.astype(jnp.bfloat16), ((0, 0), (0, tile_len - tpc)))
    packed = jnp.concatenate([own_rows, own_ids], 0)
    own_full = jnp.concatenate(
        [tiles.reshape(per_dev * tpc), jnp.full((per_dev,), -1, jnp.int32)], 0
    )
    own_lead = densify(packed[None], own_full[None], order[:lead_tiles], per_dev, tpc)
    inc_lead = gather_links(own_lead, link_devs).reshape(-1, lead)
    everyone = gather_links(packed, link_devs)
    devs = everyone.shape[0]
    ids_all = everyone[:, per_dev * tpc:, :tpc].astype(jnp.int32).reshape(devs, per_dev * tpc)
    ids_full = jnp.concatenate([ids_all, jnp.full((devs, per_dev), -1, jnp.int32)], 1)

    inc_rows = densify(
        everyone, ids_full,
        lax.dynamic_slice_in_dim(order, link_idx * row_tiles, row_tiles), per_dev, tpc,
    )
    inc_cols = densify(
        everyone, ids_full,
        lax.dynamic_slice_in_dim(order, col_idx * col_tiles, col_tiles), per_dev, tpc,
    )

    slack_ord = jnp.take(slack.reshape(ntiles, tile_len), order, axis=0).reshape(link_count)
    rows_g = link_idx * rows_dev + jnp.arange(rows_dev)
    cols_g = col_idx * cols_dev + jnp.arange(cols_dev)
    lead_g = jnp.arange(lead)

    def lead_cols(inc_x, x_g, start):
        base = contract_rows(inc_x, inc_lead)
        slack_x = lax.dynamic_slice_in_dim(slack_ord, start, x_g.shape[0])
        diag = jnp.where(x_g[:, None] == lead_g[None, :], slack_x[:, None], 0.0)
        return base + diag

    a_lead = lead_cols(inc_lead, lead_g, 0)
    f0, f1 = 0, PANEL
    l0 = jnp.linalg.cholesky(a_lead[f0:f1, f0:f1])
    inv0 = lower_inverse(l0)
    b0 = solve_rows(a_lead[f1:, f0:f1], inv0)
    head0 = jnp.concatenate([l0, b0], 0)
    rb0 = b0.astype(jnp.bfloat16)
    a11 = a_lead[f1:, f1:] - lax.dot_general(
        rb0, rb0, (((1,), (1,)), ((), ())), preferred_element_type=jnp.float32
    )
    l1 = jnp.linalg.cholesky(a11)
    inv1 = lower_inverse(l1)
    head1 = jnp.concatenate([jnp.zeros_like(l1), l1], 0)

    m_rows = lead_cols(inc_rows, rows_g, link_idx * rows_dev)
    m_cols = lead_cols(inc_cols, cols_g, col_idx * cols_dev)

    def panels(m_x, at_top):
        col0 = head_fix(solve_rows(m_x[:, f0:f1], inv0), at_top, head0)
        r0 = col0.astype(jnp.bfloat16)
        m1 = m_x[:, f1:] - lax.dot_general(
            r0, rb0, (((1,), (1,)), ((), ())), preferred_element_type=jnp.float32
        )
        col1 = head_fix(solve_rows(m1, inv1), at_top, head1)
        return col0, col1

    col0_r, col1_r = panels(m_rows, link_idx == 0)
    col0_c, col1_c = panels(m_cols, col_idx == 0)
    left_t = jnp.concatenate(
        [inc_rows, col0_r.astype(jnp.bfloat16).T, col1_r.astype(jnp.bfloat16).T], 0
    )
    right_t = jnp.concatenate(
        [inc_cols, -col0_c.astype(jnp.bfloat16).T, -col1_c.astype(jnp.bfloat16).T], 0
    )
    matrix = contract_rows(left_t, right_t)
    slack_rows = lax.dynamic_slice_in_dim(slack_ord, link_idx * rows_dev, rows_dev)
    matrix = matrix + jnp.where(
        rows_g[:, None] == cols_g[None, :], slack_rows[:, None], jnp.float32(0.0)
    )
    panel_block = jnp.concatenate([col0_r, col1_r], 1)
    padded = jnp.pad(panel_block, ((0, 0), (0, cols_dev - lead)))
    return jnp.where(
        cols_g[None, :] < lead,
        padded,
        jnp.where(rows_g[:, None] < lead, jnp.float32(0.0), matrix),
    )


def solution(mesh):
    in_specs = (P("link", None, None), P("link", None), P("link"), P(), P())
    out_specs = P("link", "col")
    return jax.shard_map(local, mesh=mesh, in_specs=in_specs, out_specs=out_specs, check_vma=False)
```

```python
import jax
import jax.numpy as jnp
from jax import lax
from jax.sharding import PartitionSpec as P

PANEL = 128
SUB = 8
HI = lax.Precision.HIGHEST


def densify(vals, ids, targets):
    groups, rows, tile_len = vals.shape
    tpc = rows // SUB
    nt = targets.shape[0]
    hits = (ids[:, None, :] == targets[None, :, None]).astype(jnp.bfloat16)
    own = (jnp.arange(SUB)[:, None] == jnp.arange(rows)[None, :] // tpc).astype(jnp.bfloat16)
    spread = (hits[:, :, None, :] * own[None, None, :, :]).reshape(groups, nt * SUB, rows)
    dense_out = lax.dot_general(
        spread, vals, (((2,), (1,)), ((0,), (0,))), preferred_element_type=jnp.float32,
    )
    dense_out = dense_out.astype(jnp.bfloat16).reshape(groups, nt, SUB, tile_len)
    return dense_out.transpose(0, 2, 1, 3).reshape(groups * SUB, nt * tile_len)


def gather_links(part, link_devs):
    cores = 2
    zs = 8
    xs = link_devs // (zs * cores)

    def shifted(block, move):
        pairs = [(src, move(src)) for src in range(link_devs)]
        return lax.ppermute(block, "link", pairs)

    def zmove(step):
        return lambda l: (l // (zs * cores)) * zs * cores + (((l // cores) % zs + step) % zs) * cores + l % cores

    def xmove(step):
        return lambda l: ((l // (zs * cores) + step) % xs) * zs * cores + l % (zs * cores)

    got = jnp.stack([part] + [shifted(part, zmove(s)) for s in range(1, zs)], 0)
    got = jnp.concatenate([got] + [shifted(got, xmove(s)) for s in range(1, xs)], 0)
    return jnp.concatenate([got, shifted(got, lambda l: l ^ 1)], 0)


def contract_rows(left_side, right_side):
    return lax.dot_general(
        left_side, right_side, (((0,), (0,)), ((), ())), preferred_element_type=jnp.float32
    )


def lower_inverse(lower):
    eye = jnp.eye(lower.shape[0], dtype=jnp.float32)
    return jax.scipy.linalg.solve_triangular(lower, eye, lower=True)


def solve_rows(block, inv_lower):
    return lax.dot_general(
        block, inv_lower, (((1,), (1,)), ((), ())), precision=HI,
        preferred_element_type=jnp.float32,
    )


def head_fix(solved, at_top, head):
    top = jnp.where(at_top, head, solved[: head.shape[0]])
    return jnp.concatenate([top, solved[head.shape[0]:]], 0)


def local(values, tiles, barrier, slack, order):
    link_devs = lax.axis_size("link")
    col_devs = lax.axis_size("col")
    link_idx = lax.axis_index("link")
    col_idx = lax.axis_index("col")
    link_count = slack.shape[0]
    rows_dev = link_count // link_devs
    cols_dev = link_count // col_devs
    per_dev, tpc, tile_len = values.shape
    ntiles = order.shape[0]
    lead = 2 * PANEL
    lead_tiles = lead // tile_len
    row_tiles = rows_dev // tile_len
    col_tiles = cols_dev // tile_len
    factor = link_count / (per_dev * link_devs * tpc * tile_len)
    scaled = (jnp.sqrt(barrier * factor)[:, None, None] * values.astype(jnp.float32)).astype(
        jnp.bfloat16
    )
    own_rows = scaled.reshape(per_dev * tpc, tile_len)
    own_ids = jnp.pad(tiles.astype(jnp.bfloat16), ((0, 0), (0, tile_len - tpc)))
    packed = jnp.concatenate([own_rows, own_ids], 0)
    groups = per_dev // SUB
    own_lead = densify(
        own_rows.reshape(groups, SUB * tpc, tile_len), tiles.reshape(groups, SUB * tpc),
        order[:lead_tiles],
    )
    copies = jnp.broadcast_to(own_lead[None], (link_devs,) + own_lead.shape)
    inc_lead = lax.all_to_all(copies, "link", 0, 0, tiled=True).reshape(-1, lead)
    everyone = lax.all_gather(packed, "link", axis=0)
    devs = everyone.shape[0]
    ids_all = everyone[:, per_dev * tpc:, :tpc].astype(jnp.int32)
    ids_all = ids_all.reshape(devs * groups, SUB * tpc)
    vals_all = everyone[:, : per_dev * tpc].reshape(devs * groups, SUB * tpc, tile_len)

    inc_rows = densify(
        vals_all, ids_all, lax.dynamic_slice_in_dim(order, link_idx * row_tiles, row_tiles)
    )
    inc_cols = densify(
        vals_all, ids_all, lax.dynamic_slice_in_dim(order, col_idx * col_tiles, col_tiles)
    )

    slack_ord = jnp.take(slack.reshape(ntiles, tile_len), order, axis=0).reshape(link_count)
    rows_g = link_idx * rows_dev + jnp.arange(rows_dev)
    cols_g = col_idx * cols_dev + jnp.arange(cols_dev)
    lead_g = jnp.arange(lead)

    def lead_cols(inc_x, x_g, start):
        base = contract_rows(inc_x, inc_lead)
        slack_x = lax.dynamic_slice_in_dim(slack_ord, start, x_g.shape[0])
        diag = jnp.where(x_g[:, None] == lead_g[None, :], slack_x[:, None], 0.0)
        return base + diag

    a_lead = lead_cols(inc_lead, lead_g, 0)
    f0, f1 = 0, PANEL
    l0 = jnp.linalg.cholesky(a_lead[f0:f1, f0:f1])
    inv0 = lower_inverse(l0)
    b0 = solve_rows(a_lead[f1:, f0:f1], inv0)
    head0 = jnp.concatenate([l0, b0], 0)
    rb0 = b0.astype(jnp.bfloat16)
    a11 = a_lead[f1:, f1:] - lax.dot_general(
        rb0, rb0, (((1,), (1,)), ((), ())), preferred_element_type=jnp.float32
    )
    l1 = jnp.linalg.cholesky(a11)
    inv1 = lower_inverse(l1)
    head1 = jnp.concatenate([jnp.zeros_like(l1), l1], 0)

    m_rows = lead_cols(inc_rows, rows_g, link_idx * rows_dev)
    m_cols = lead_cols(inc_cols, cols_g, col_idx * cols_dev)

    def panels(m_x, at_top):
        col0 = head_fix(solve_rows(m_x[:, f0:f1], inv0), at_top, head0)
        r0 = col0.astype(jnp.bfloat16)
        m1 = m_x[:, f1:] - lax.dot_general(
            r0, rb0, (((1,), (1,)), ((), ())), preferred_element_type=jnp.float32
        )
        col1 = head_fix(solve_rows(m1, inv1), at_top, head1)
        return col0, col1

    col0_r, col1_r = panels(m_rows, link_idx == 0)
    col0_c, col1_c = panels(m_cols, col_idx == 0)
    left_t = jnp.concatenate(
        [inc_rows, col0_r.astype(jnp.bfloat16).T, col1_r.astype(jnp.bfloat16).T], 0
    )
    right_t = jnp.concatenate(
        [inc_cols, -col0_c.astype(jnp.bfloat16).T, -col1_c.astype(jnp.bfloat16).T], 0
    )
    matrix = contract_rows(left_t, right_t)
    slack_rows = lax.dynamic_slice_in_dim(slack_ord, link_idx * rows_dev, rows_dev)
    matrix = matrix + jnp.where(
        rows_g[:, None] == cols_g[None, :], slack_rows[:, None], jnp.float32(0.0)
    )
    panel_block = jnp.concatenate([col0_r, col1_r], 1)
    padded = jnp.pad(panel_block, ((0, 0), (0, cols_dev - lead)))
    return jnp.where(
        cols_g[None, :] < lead,
        padded,
        jnp.where(rows_g[:, None] < lead, jnp.float32(0.0), matrix),
    )


def solution(mesh):
    in_specs = (P("link", None, None), P("link", None), P("link"), P(), P())
    out_specs = P("link", "col")
    return jax.shard_map(local, mesh=mesh, in_specs=in_specs, out_specs=out_specs, check_vma=False)
```

```python
import jax
import jax.numpy as jnp
from jax import lax
from jax.sharding import PartitionSpec as P

PANEL = 128
SUB = 8
HI = lax.Precision.HIGHEST


def densify(vals, ids, targets):
    groups, rows, tile_len = vals.shape
    tpc = rows // SUB
    nt = targets.shape[0]
    hits = (ids[:, None, :] == targets[None, :, None]).astype(jnp.bfloat16)
    own = (jnp.arange(SUB)[:, None] == jnp.arange(rows)[None, :] // tpc).astype(jnp.bfloat16)
    spread = (hits[:, :, None, :] * own[None, None, :, :]).reshape(groups, nt * SUB, rows)
    dense_out = lax.dot_general(
        spread, vals, (((2,), (1,)), ((0,), (0,))), preferred_element_type=jnp.float32,
    )
    dense_out = dense_out.astype(jnp.bfloat16).reshape(groups, nt, SUB, tile_len)
    return dense_out.transpose(0, 2, 1, 3).reshape(groups * SUB, nt * tile_len)


def gather_links(part, link_devs):
    cores = 2
    zs = 8
    xs = link_devs // (zs * cores)

    def shifted(block, move):
        pairs = [(src, move(src)) for src in range(link_devs)]
        return lax.ppermute(block, "link", pairs)

    def zmove(step):
        return lambda l: (l // (zs * cores)) * zs * cores + (((l // cores) % zs + step) % zs) * cores + l % cores

    def xmove(step):
        return lambda l: ((l // (zs * cores) + step) % xs) * zs * cores + l % (zs * cores)

    got = jnp.stack([part] + [shifted(part, zmove(s)) for s in range(1, zs)], 0)
    got = jnp.concatenate([got] + [shifted(got, xmove(s)) for s in range(1, xs)], 0)
    got = jnp.concatenate([got, shifted(got, lambda l: l ^ 1)], 0)
    me = lax.axis_index("link")
    block = jnp.arange(link_devs)
    zsrc = ((me // cores) % zs - block % zs) % zs
    xsrc = (me // (zs * cores) - (block // zs) % xs) % xs
    csrc = (me % cores) ^ (block // (zs * xs))
    return got, xsrc * zs * cores + zsrc * cores + csrc


def contract_rows(left_side, right_side):
    return lax.dot_general(
        left_side, right_side, (((0,), (0,)), ((), ())), preferred_element_type=jnp.float32
    )


def lower_inverse(lower):
    eye = jnp.eye(lower.shape[0], dtype=jnp.float32)
    return jax.scipy.linalg.solve_triangular(lower, eye, lower=True)


def solve_rows(block, inv_lower):
    return lax.dot_general(
        block, inv_lower, (((1,), (1,)), ((), ())), precision=HI,
        preferred_element_type=jnp.float32,
    )


def head_fix(solved, at_top, head):
    top = jnp.where(at_top, head, solved[: head.shape[0]])
    return jnp.concatenate([top, solved[head.shape[0]:]], 0)


def local(values, tiles, barrier, slack, order):
    link_devs = lax.axis_size("link")
    col_devs = lax.axis_size("col")
    link_idx = lax.axis_index("link")
    col_idx = lax.axis_index("col")
    link_count = slack.shape[0]
    rows_dev = link_count // link_devs
    cols_dev = link_count // col_devs
    per_dev, tpc, tile_len = values.shape
    ntiles = order.shape[0]
    lead = 2 * PANEL
    lead_tiles = lead // tile_len
    row_tiles = rows_dev // tile_len
    col_tiles = cols_dev // tile_len
    factor = link_count / (per_dev * link_devs * tpc * tile_len)
    scaled = (jnp.sqrt(barrier * factor)[:, None, None] * values.astype(jnp.float32)).astype(
        jnp.bfloat16
    )
    own_rows = scaled.reshape(per_dev * tpc, tile_len)
    groups = per_dev // SUB
    own_lead = densify(
        own_rows.reshape(groups, SUB * tpc, tile_len), tiles.reshape(groups, SUB * tpc),
        order[:lead_tiles],
    )
    own_ids = jnp.pad(tiles.astype(jnp.bfloat16), ((0, 0), (0, tile_len - tpc)))
    small = jnp.concatenate([own_lead, own_ids], 1)
    copies = jnp.broadcast_to(small[None], (link_devs,) + small.shape)
    small_all = lax.all_to_all(copies, "link", 0, 0, tiled=True).reshape(-1, lead + tile_len)
    everyone, sources = gather_links(own_rows, link_devs)
    devs = everyone.shape[0]
    pick = (sources[:, None] == jnp.arange(link_devs)[None, :]).astype(jnp.bfloat16)
    small_all = jnp.dot(
        pick, small_all.reshape(link_devs, -1), preferred_element_type=jnp.float32
    ).astype(jnp.bfloat16).reshape(-1, lead + tile_len)
    inc_lead = small_all[:, :lead]
    ids_all = small_all[:, lead : lead + tpc].astype(jnp.int32)
    ids_all = ids_all.reshape(devs * groups, SUB * tpc)
    vals_all = everyone.reshape(devs * groups, SUB * tpc, tile_len)

    inc_rows = densify(
        vals_all, ids_all, lax.dynamic_slice_in_dim(order, link_idx * row_tiles, row_tiles)
    )
    inc_cols = densify(
        vals_all, ids_all, lax.dynamic_slice_in_dim(order, col_idx * col_tiles, col_tiles)
    )

    slack_ord = jnp.take(slack.reshape(ntiles, tile_len), order, axis=0).reshape(link_count)
    rows_g = link_idx * rows_dev + jnp.arange(rows_dev)
    cols_g = col_idx * cols_dev + jnp.arange(cols_dev)
    lead_g = jnp.arange(lead)

    def lead_cols(inc_x, x_g, start):
        base = contract_rows(inc_x, inc_lead)
        slack_x = lax.dynamic_slice_in_dim(slack_ord, start, x_g.shape[0])
        diag = jnp.where(x_g[:, None] == lead_g[None, :], slack_x[:, None], 0.0)
        return base + diag

    a_lead = lead_cols(inc_lead, lead_g, 0)
    f0, f1 = 0, PANEL
    l0 = jnp.linalg.cholesky(a_lead[f0:f1, f0:f1])
    inv0 = lower_inverse(l0)
    b0 = solve_rows(a_lead[f1:, f0:f1], inv0)
    head0 = jnp.concatenate([l0, b0], 0)
    rb0 = b0.astype(jnp.bfloat16)
    a11 = a_lead[f1:, f1:] - lax.dot_general(
        rb0, rb0, (((1,), (1,)), ((), ())), preferred_element_type=jnp.float32
    )
    l1 = jnp.linalg.cholesky(a11)
    inv1 = lower_inverse(l1)
    head1 = jnp.concatenate([jnp.zeros_like(l1), l1], 0)

    m_rows = lead_cols(inc_rows, rows_g, link_idx * rows_dev)
    m_cols = lead_cols(inc_cols, cols_g, col_idx * cols_dev)

    def panels(m_x, at_top):
        col0 = head_fix(solve_rows(m_x[:, f0:f1], inv0), at_top, head0)
        r0 = col0.astype(jnp.bfloat16)
        m1 = m_x[:, f1:] - lax.dot_general(
            r0, rb0, (((1,), (1,)), ((), ())), preferred_element_type=jnp.float32
        )
        col1 = head_fix(solve_rows(m1, inv1), at_top, head1)
        return col0, col1

    col0_r, col1_r = panels(m_rows, link_idx == 0)
    col0_c, col1_c = panels(m_cols, col_idx == 0)
    left_t = jnp.concatenate(
        [inc_rows, col0_r.astype(jnp.bfloat16).T, col1_r.astype(jnp.bfloat16).T], 0
    )
    right_t = jnp.concatenate(
        [inc_cols, -col0_c.astype(jnp.bfloat16).T, -col1_c.astype(jnp.bfloat16).T], 0
    )
    matrix = contract_rows(left_t, right_t)
    slack_rows = lax.dynamic_slice_in_dim(slack_ord, link_idx * rows_dev, rows_dev)
    matrix = matrix + jnp.where(
        rows_g[:, None] == cols_g[None, :], slack_rows[:, None], jnp.float32(0.0)
    )
    panel_block = jnp.concatenate([col0_r, col1_r], 1)
    padded = jnp.pad(panel_block, ((0, 0), (0, cols_dev - lead)))
    return jnp.where(
        cols_g[None, :] < lead,
        padded,
        jnp.where(rows_g[:, None] < lead, jnp.float32(0.0), matrix),
    )


def solution(mesh):
    in_specs = (P("link", None, None), P("link", None), P("link"), P(), P())
    out_specs = P("link", "col")
    return jax.shard_map(local, mesh=mesh, in_specs=in_specs, out_specs=out_specs, check_vma=False)
```

```python
import jax
import jax.numpy as jnp
from jax import lax
from jax.sharding import PartitionSpec as P

PANEL = 128
SUB = 8
HI = lax.Precision.HIGHEST


def densify(vals, ids, targets):
    groups, rows, tile_len = vals.shape
    tpc = rows // SUB
    nt = targets.shape[0]
    hits = (ids[:, None, :] == targets[None, :, None]).astype(jnp.bfloat16)
    own = (jnp.arange(SUB)[:, None] == jnp.arange(rows)[None, :] // tpc).astype(jnp.bfloat16)
    spread = (hits[:, :, None, :] * own[None, None, :, :]).reshape(groups, nt * SUB, rows)
    dense_out = lax.dot_general(
        spread, vals, (((2,), (1,)), ((0,), (0,))), preferred_element_type=jnp.float32,
    )
    dense_out = dense_out.astype(jnp.bfloat16).reshape(groups, nt, SUB, tile_len)
    return dense_out.transpose(0, 2, 1, 3).reshape(groups * SUB, nt * tile_len)


def gather_links(part, link_devs):
    cores = 2
    zs = 8
    xs = link_devs // (zs * cores)

    def shifted(block, move):
        pairs = [(src, move(src)) for src in range(link_devs)]
        return lax.ppermute(block, "link", pairs)

    def zmove(step):
        return lambda l: (l // (zs * cores)) * zs * cores + (((l // cores) % zs + step) % zs) * cores + l % cores

    def xmove(step):
        return lambda l: ((l // (zs * cores) + step) % xs) * zs * cores + l % (zs * cores)

    got = jnp.stack([part] + [shifted(part, zmove(s)) for s in range(1, zs)], 0)
    got = jnp.concatenate([got] + [shifted(got, xmove(s)) for s in range(1, xs)], 0)
    got = jnp.concatenate([got, shifted(got, lambda l: l ^ 1)], 0)
    me = lax.axis_index("link")
    block = jnp.arange(link_devs)
    zsrc = ((me // cores) % zs - block % zs) % zs
    xsrc = (me // (zs * cores) - (block // zs) % xs) % xs
    csrc = (me % cores) ^ (block // (zs * xs))
    return got, xsrc * zs * cores + zsrc * cores + csrc


def contract_rows(left_side, right_side):
    return lax.dot_general(
        left_side, right_side, (((0,), (0,)), ((), ())), preferred_element_type=jnp.float32
    )


def lower_inverse(lower):
    eye = jnp.eye(lower.shape[0], dtype=jnp.float32)
    return jax.scipy.linalg.solve_triangular(lower, eye, lower=True)


def solve_rows(block, inv_lower):
    return lax.dot_general(
        block, inv_lower, (((1,), (1,)), ((), ())), precision=HI,
        preferred_element_type=jnp.float32,
    )


def head_fix(solved, at_top, head):
    top = jnp.where(at_top, head, solved[: head.shape[0]])
    return jnp.concatenate([top, solved[head.shape[0]:]], 0)


def local(values, tiles, barrier, slack, order):
    link_devs = lax.axis_size("link")
    col_devs = lax.axis_size("col")
    link_idx = lax.axis_index("link")
    col_idx = lax.axis_index("col")
    link_count = slack.shape[0]
    rows_dev = link_count // link_devs
    cols_dev = link_count // col_devs
    per_dev, tpc, tile_len = values.shape
    ntiles = order.shape[0]
    lead = 2 * PANEL
    lead_tiles = lead // tile_len
    row_tiles = rows_dev // tile_len
    col_tiles = cols_dev // tile_len
    factor = link_count / (per_dev * link_devs * tpc * tile_len)
    scaled = (jnp.sqrt(barrier * factor)[:, None, None] * values.astype(jnp.float32)).astype(
        jnp.bfloat16
    )
    own_rows = scaled.reshape(per_dev * tpc, tile_len)
    groups = per_dev // SUB
    own_lead = densify(
        own_rows.reshape(groups, SUB * tpc, tile_len), tiles.reshape(groups, SUB * tpc),
        order[:lead_tiles],
    )
    own_ids = jnp.pad(tiles.astype(jnp.bfloat16), ((0, 0), (0, tile_len - tpc)))
    small = jnp.concatenate([own_lead, own_ids], 1)
    small_all, _ = gather_links(small, link_devs)
    small_all = small_all.reshape(-1, lead + tile_len)
    everyone, _ = gather_links(own_rows, link_devs)
    devs = everyone.shape[0]
    inc_lead = small_all[:, :lead]
    ids_all = small_all[:, lead : lead + tpc].astype(jnp.int32)
    ids_all = ids_all.reshape(devs * groups, SUB * tpc)
    vals_all = everyone.reshape(devs * groups, SUB * tpc, tile_len)

    inc_rows = densify(
        vals_all, ids_all, lax.dynamic_slice_in_dim(order, link_idx * row_tiles, row_tiles)
    )
    inc_cols = densify(
        vals_all, ids_all, lax.dynamic_slice_in_dim(order, col_idx * col_tiles, col_tiles)
    )

    slack_ord = jnp.take(slack.reshape(ntiles, tile_len), order, axis=0).reshape(link_count)
    rows_g = link_idx * rows_dev + jnp.arange(rows_dev)
    cols_g = col_idx * cols_dev + jnp.arange(cols_dev)
    lead_g = jnp.arange(lead)

    def lead_cols(inc_x, x_g, start):
        base = contract_rows(inc_x, inc_lead)
        slack_x = lax.dynamic_slice_in_dim(slack_ord, start, x_g.shape[0])
        diag = jnp.where(x_g[:, None] == lead_g[None, :], slack_x[:, None], 0.0)
        return base + diag

    a_lead = lead_cols(inc_lead, lead_g, 0)
    f0, f1 = 0, PANEL
    l0 = jnp.linalg.cholesky(a_lead[f0:f1, f0:f1])
    inv0 = lower_inverse(l0)
    b0 = solve_rows(a_lead[f1:, f0:f1], inv0)
    head0 = jnp.concatenate([l0, b0], 0)
    rb0 = b0.astype(jnp.bfloat16)
    a11 = a_lead[f1:, f1:] - lax.dot_general(
        rb0, rb0, (((1,), (1,)), ((), ())), preferred_element_type=jnp.float32
    )
    l1 = jnp.linalg.cholesky(a11)
    inv1 = lower_inverse(l1)
    head1 = jnp.concatenate([jnp.zeros_like(l1), l1], 0)

    m_rows = lead_cols(inc_rows, rows_g, link_idx * rows_dev)
    m_cols = lead_cols(inc_cols, cols_g, col_idx * cols_dev)

    def panels(m_x, at_top):
        col0 = head_fix(solve_rows(m_x[:, f0:f1], inv0), at_top, head0)
        r0 = col0.astype(jnp.bfloat16)
        m1 = m_x[:, f1:] - lax.dot_general(
            r0, rb0, (((1,), (1,)), ((), ())), preferred_element_type=jnp.float32
        )
        col1 = head_fix(solve_rows(m1, inv1), at_top, head1)
        return col0, col1

    col0_r, col1_r = panels(m_rows, link_idx == 0)
    col0_c, col1_c = panels(m_cols, col_idx == 0)
    left_t = jnp.concatenate(
        [inc_rows, col0_r.astype(jnp.bfloat16).T, col1_r.astype(jnp.bfloat16).T], 0
    )
    right_t = jnp.concatenate(
        [inc_cols, -col0_c.astype(jnp.bfloat16).T, -col1_c.astype(jnp.bfloat16).T], 0
    )
    matrix = contract_rows(left_t, right_t)
    slack_rows = lax.dynamic_slice_in_dim(slack_ord, link_idx * rows_dev, rows_dev)
    matrix = matrix + jnp.where(
        rows_g[:, None] == cols_g[None, :], slack_rows[:, None], jnp.float32(0.0)
    )
    panel_block = jnp.concatenate([col0_r, col1_r], 1)
    padded = jnp.pad(panel_block, ((0, 0), (0, cols_dev - lead)))
    return jnp.where(
        cols_g[None, :] < lead,
        padded,
        jnp.where(rows_g[:, None] < lead, jnp.float32(0.0), matrix),
    )


def solution(mesh):
    in_specs = (P("link", None, None), P("link", None), P("link"), P(), P())
    out_specs = P("link", "col")
    return jax.shard_map(local, mesh=mesh, in_specs=in_specs, out_specs=out_specs, check_vma=False)
```

```python
import jax
import jax.numpy as jnp
from jax import lax
from jax.sharding import PartitionSpec as P

PANEL = 128
SUB = 8
HI = lax.Precision.HIGHEST


def densify(vals, ids, targets):
    groups, rows, tile_len = vals.shape
    tpc = rows // SUB
    nt = targets.shape[0]
    hits = (ids[:, None, :] == targets[None, :, None]).astype(jnp.bfloat16)
    own = (jnp.arange(SUB)[:, None] == jnp.arange(rows)[None, :] // tpc).astype(jnp.bfloat16)
    spread = (hits[:, :, None, :] * own[None, None, :, :]).reshape(groups, nt * SUB, rows)
    dense_out = lax.dot_general(
        spread, vals, (((2,), (1,)), ((0,), (0,))), preferred_element_type=jnp.float32,
    )
    dense_out = dense_out.astype(jnp.bfloat16).reshape(groups, nt, SUB, tile_len)
    return dense_out.transpose(0, 2, 1, 3).reshape(groups * SUB, nt * tile_len)


def gather_links(part, link_devs):
    cores = 2
    zs = 8
    xs = link_devs // (zs * cores)

    def shifted(block, move):
        pairs = [(src, move(src)) for src in range(link_devs)]
        return lax.ppermute(block, "link", pairs)

    def zmove(step):
        return lambda l: (l // (zs * cores)) * zs * cores + (((l // cores) % zs + step) % zs) * cores + l % cores

    def xmove(step):
        return lambda l: ((l // (zs * cores) + step) % xs) * zs * cores + l % (zs * cores)

    got = jnp.stack([part] + [shifted(part, zmove(s)) for s in range(1, zs)], 0)
    got = jnp.concatenate([got] + [shifted(got, xmove(s)) for s in range(1, xs)], 0)
    return jnp.concatenate([got, shifted(got, lambda l: l ^ 1)], 0)


def contract_rows(left_side, right_side):
    return lax.dot_general(
        left_side, right_side, (((0,), (0,)), ((), ())), preferred_element_type=jnp.float32
    )


def lower_inverse(lower):
    eye = jnp.eye(lower.shape[0], dtype=jnp.float32)
    return jax.scipy.linalg.solve_triangular(lower, eye, lower=True)


def solve_rows(block, inv_lower):
    return lax.dot_general(
        block, inv_lower, (((1,), (1,)), ((), ())), precision=HI,
        preferred_element_type=jnp.float32,
    )


def head_fix(solved, at_top, head):
    top = jnp.where(at_top, head, solved[: head.shape[0]])
    return jnp.concatenate([top, solved[head.shape[0]:]], 0)


def local(values, tiles, barrier, slack, order):
    link_devs = lax.axis_size("link")
    col_devs = lax.axis_size("col")
    link_idx = lax.axis_index("link")
    col_idx = lax.axis_index("col")
    link_count = slack.shape[0]
    rows_dev = link_count // link_devs
    cols_dev = link_count // col_devs
    per_dev, tpc, tile_len = values.shape
    ntiles = order.shape[0]
    lead = 2 * PANEL
    lead_tiles = lead // tile_len
    row_tiles = rows_dev // tile_len
    col_tiles = cols_dev // tile_len
    factor = link_count / (per_dev * link_devs * tpc * tile_len)
    scaled = (jnp.sqrt(barrier * factor)[:, None, None] * values.astype(jnp.float32)).astype(
        jnp.bfloat16
    )
    own_rows = scaled.reshape(per_dev * tpc, tile_len)
    groups = per_dev // SUB
    own_lead = densify(
        own_rows.reshape(groups, SUB * tpc, tile_len), tiles.reshape(groups, SUB * tpc),
        order[:lead_tiles],
    )
    own_ids = jnp.pad(tiles.astype(jnp.bfloat16), ((0, 0), (0, tile_len - tpc)))
    small = jnp.concatenate([own_lead, own_ids], 1)
    copies = jnp.broadcast_to(small[None], (link_devs,) + small.shape)
    small_all = lax.all_to_all(copies, "link", 0, 0, tiled=True).reshape(-1, lead + tile_len)
    inc_lead = small_all[:, :lead]
    everyone = lax.all_gather(own_rows, "link", axis=0)
    devs = everyone.shape[0]
    ids_all = small_all[:, lead : lead + tpc].astype(jnp.int32)
    ids_all = ids_all.reshape(devs * groups, SUB * tpc)
    vals_all = everyone.reshape(devs * groups, SUB * tpc, tile_len)

    inc_rows = densify(
        vals_all, ids_all, lax.dynamic_slice_in_dim(order, link_idx * row_tiles, row_tiles)
    )
    inc_cols = densify(
        vals_all, ids_all, lax.dynamic_slice_in_dim(order, col_idx * col_tiles, col_tiles)
    )

    slack_ord = jnp.take(slack.reshape(ntiles, tile_len), order, axis=0).reshape(link_count)
    rows_g = link_idx * rows_dev + jnp.arange(rows_dev)
    cols_g = col_idx * cols_dev + jnp.arange(cols_dev)
    lead_g = jnp.arange(lead)

    def lead_cols(inc_x, x_g, start):
        base = contract_rows(inc_x, inc_lead)
        slack_x = lax.dynamic_slice_in_dim(slack_ord, start, x_g.shape[0])
        diag = jnp.where(x_g[:, None] == lead_g[None, :], slack_x[:, None], 0.0)
        return base + diag

    a_lead = lead_cols(inc_lead, lead_g, 0)
    f0, f1 = 0, PANEL
    l0 = jnp.linalg.cholesky(a_lead[f0:f1, f0:f1])
    inv0 = lower_inverse(l0)
    b0 = solve_rows(a_lead[f1:, f0:f1], inv0)
    head0 = jnp.concatenate([l0, b0], 0)
    rb0 = b0.astype(jnp.bfloat16)
    a11 = a_lead[f1:, f1:] - lax.dot_general(
        rb0, rb0, (((1,), (1,)), ((), ())), preferred_element_type=jnp.float32
    )
    l1 = jnp.linalg.cholesky(a11)
    inv1 = lower_inverse(l1)
    head1 = jnp.concatenate([jnp.zeros_like(l1), l1], 0)

    m_rows = lead_cols(inc_rows, rows_g, link_idx * rows_dev)
    m_cols = lead_cols(inc_cols, cols_g, col_idx * cols_dev)

    def panels(m_x, at_top):
        col0 = head_fix(solve_rows(m_x[:, f0:f1], inv0), at_top, head0)
        r0 = col0.astype(jnp.bfloat16)
        m1 = m_x[:, f1:] - lax.dot_general(
            r0, rb0, (((1,), (1,)), ((), ())), preferred_element_type=jnp.float32
        )
        col1 = head_fix(solve_rows(m1, inv1), at_top, head1)
        return col0, col1

    col0_r, col1_r = panels(m_rows, link_idx == 0)
    col0_c, col1_c = panels(m_cols, col_idx == 0)
    left_t = jnp.concatenate(
        [inc_rows, col0_r.astype(jnp.bfloat16).T, col1_r.astype(jnp.bfloat16).T], 0
    )
    right_t = jnp.concatenate(
        [inc_cols, -col0_c.astype(jnp.bfloat16).T, -col1_c.astype(jnp.bfloat16).T], 0
    )
    matrix = contract_rows(left_t, right_t)
    slack_rows = lax.dynamic_slice_in_dim(slack_ord, link_idx * rows_dev, rows_dev)
    matrix = matrix + jnp.where(
        rows_g[:, None] == cols_g[None, :], slack_rows[:, None], jnp.float32(0.0)
    )
    panel_block = jnp.concatenate([col0_r, col1_r], 1)
    padded = jnp.pad(panel_block, ((0, 0), (0, cols_dev - lead)))
    return jnp.where(
        cols_g[None, :] < lead,
        padded,
        jnp.where(rows_g[:, None] < lead, jnp.float32(0.0), matrix),
    )


def solution(mesh):
    in_specs = (P("link", None, None), P("link", None), P("link"), P(), P())
    out_specs = P("link", "col")
    return jax.shard_map(local, mesh=mesh, in_specs=in_specs, out_specs=out_specs, check_vma=False)
```

```python
import jax
import jax.numpy as jnp
from jax import lax
from jax.sharding import PartitionSpec as P
from jax.experimental import pallas as pl
from jax.experimental.pallas import tpu as pltpu

PANEL = 128
SUB = 8
HI = lax.Precision.HIGHEST
BLK = 8


def _chol_inv_kernel(a_ref, lt_ref, inv_ref, work, binv):
    n = a_ref.shape[0]
    work[...] = a_ref[...]
    rr = lax.broadcasted_iota(jnp.int32, (n, n), 0)
    cc = lax.broadcasted_iota(jnp.int32, (n, n), 1)
    binv[...] = jnp.where(rr == cc, 1.0, 0.0).astype(jnp.float32)
    lane = lax.broadcasted_iota(jnp.int32, (BLK, n), 1)
    sub = lax.broadcasted_iota(jnp.int32, (BLK, n), 0)
    subc = lax.broadcasted_iota(jnp.int32, (BLK, 1), 0)

    def block(b, carry):
        base = pl.multiple_of(b * BLK, BLK)
        slab = work[pl.ds(base, BLK), :]
        bslab = binv[pl.ds(base, BLK), :]
        out = jnp.zeros((BLK, n), jnp.float32)
        xout = jnp.zeros((BLK, n), jnp.float32)
        for i in range(BLK):
            col = base + i
            rowi = jnp.sum(jnp.where(sub == i, slab, 0.0), axis=0, keepdims=True)
            d = jnp.sum(jnp.where(lane[0:1] == col, rowi, 0.0), axis=1, keepdims=True)
            s = 1.0 / jnp.sqrt(d)
            lrow = jnp.where(lane[0:1] >= col, rowi * s, 0.0)
            out = jnp.where(sub == i, lrow, out)
            colv = jnp.sum(jnp.where(lane == col, slab, 0.0), axis=1, keepdims=True) * s
            slab = slab - colv * lrow
            xi = jnp.sum(jnp.where(sub == i, bslab, 0.0), axis=0, keepdims=True) * s
            xout = jnp.where(sub == i, xi, xout)
            bslab = bslab - jnp.where(subc > i, colv, 0.0) * xi
        lt_ref[pl.ds(base, BLK), :] = out
        inv_ref[pl.ds(base, BLK), :] = xout
        out_t = out.T
        work[...] = work[...] - jnp.dot(out_t, out, precision=HI, preferred_element_type=jnp.float32)
        binv[...] = binv[...] - jnp.dot(out_t, xout, precision=HI, preferred_element_type=jnp.float32)
        return carry

    lax.fori_loop(0, n // BLK, block, 0)


def chol_inv(a):
    n = a.shape[0]
    lt, inv = pl.pallas_call(
        _chol_inv_kernel,
        out_shape=(jax.ShapeDtypeStruct((n, n), jnp.float32), jax.ShapeDtypeStruct((n, n), jnp.float32)),
        scratch_shapes=[pltpu.VMEM((n, n), jnp.float32), pltpu.VMEM((n, n), jnp.float32)],
    )(a)
    return lt.T, inv


def densify(vals, ids, targets):
    groups, rows, tile_len = vals.shape
    tpc = rows // SUB
    nt = targets.shape[0]
    hits = (ids[:, None, :] == targets[None, :, None]).astype(jnp.bfloat16)
    own = (jnp.arange(SUB)[:, None] == jnp.arange(rows)[None, :] // tpc).astype(jnp.bfloat16)
    spread = (hits[:, :, None, :] * own[None, None, :, :]).reshape(groups, nt * SUB, rows)
    dense_out = lax.dot_general(
        spread, vals, (((2,), (1,)), ((0,), (0,))), preferred_element_type=jnp.float32,
    )
    dense_out = dense_out.astype(jnp.bfloat16).reshape(groups, nt, SUB, tile_len)
    return dense_out.transpose(0, 2, 1, 3).reshape(groups * SUB, nt * tile_len)


def gather_links(part, link_devs):
    cores = 2
    zs = 8
    xs = link_devs // (zs * cores)

    def shifted(block, move):
        pairs = [(src, move(src)) for src in range(link_devs)]
        return lax.ppermute(block, "link", pairs)

    def zmove(step):
        return lambda l: (l // (zs * cores)) * zs * cores + (((l // cores) % zs + step) % zs) * cores + l % cores

    def xmove(step):
        return lambda l: ((l // (zs * cores) + step) % xs) * zs * cores + l % (zs * cores)

    got = jnp.stack([part] + [shifted(part, zmove(s)) for s in range(1, zs)], 0)
    got = jnp.concatenate([got] + [shifted(got, xmove(s)) for s in range(1, xs)], 0)
    return jnp.concatenate([got, shifted(got, lambda l: l ^ 1)], 0)


def contract_rows(left_side, right_side):
    return lax.dot_general(
        left_side, right_side, (((0,), (0,)), ((), ())), preferred_element_type=jnp.float32
    )


def lower_inverse(lower):
    eye = jnp.eye(lower.shape[0], dtype=jnp.float32)
    return jax.scipy.linalg.solve_triangular(lower, eye, lower=True)


def solve_rows(block, inv_lower):
    return lax.dot_general(
        block, inv_lower, (((1,), (1,)), ((), ())), precision=HI,
        preferred_element_type=jnp.float32,
    )


def head_fix(solved, at_top, head):
    top = jnp.where(at_top, head, solved[: head.shape[0]])
    return jnp.concatenate([top, solved[head.shape[0]:]], 0)


def local(values, tiles, barrier, slack, order):
    link_devs = lax.axis_size("link")
    col_devs = lax.axis_size("col")
    link_idx = lax.axis_index("link")
    col_idx = lax.axis_index("col")
    link_count = slack.shape[0]
    rows_dev = link_count // link_devs
    cols_dev = link_count // col_devs
    per_dev, tpc, tile_len = values.shape
    ntiles = order.shape[0]
    lead = 2 * PANEL
    lead_tiles = lead // tile_len
    row_tiles = rows_dev // tile_len
    col_tiles = cols_dev // tile_len
    factor = link_count / (per_dev * link_devs * tpc * tile_len)
    scaled = (jnp.sqrt(barrier * factor)[:, None, None] * values.astype(jnp.float32)).astype(
        jnp.bfloat16
    )
    own_rows = scaled.reshape(per_dev * tpc, tile_len)
    groups = per_dev // SUB
    own_lead = densify(
        own_rows.reshape(groups, SUB * tpc, tile_len), tiles.reshape(groups, SUB * tpc),
        order[:lead_tiles],
    )
    own_ids = jnp.pad(tiles.astype(jnp.bfloat16), ((0, 0), (0, tile_len - tpc)))
    small = jnp.concatenate([own_lead, own_ids], 1)
    copies = jnp.broadcast_to(small[None], (link_devs,) + small.shape)
    small_all = lax.all_to_all(copies, "link", 0, 0, tiled=True).reshape(-1, lead + tile_len)
    inc_lead = small_all[:, :lead]
    everyone = lax.all_gather(own_rows, "link", axis=0)
    devs = everyone.shape[0]
    ids_all = small_all[:, lead : lead + tpc].astype(jnp.int32)
    ids_all = ids_all.reshape(devs * groups, SUB * tpc)
    vals_all = everyone.reshape(devs * groups, SUB * tpc, tile_len)

    inc_rows = densify(
        vals_all, ids_all, lax.dynamic_slice_in_dim(order, link_idx * row_tiles, row_tiles)
    )
    inc_cols = densify(
        vals_all, ids_all, lax.dynamic_slice_in_dim(order, col_idx * col_tiles, col_tiles)
    )

    slack_ord = jnp.take(slack.reshape(ntiles, tile_len), order, axis=0).reshape(link_count)
    rows_g = link_idx * rows_dev + jnp.arange(rows_dev)
    cols_g = col_idx * cols_dev + jnp.arange(cols_dev)
    lead_g = jnp.arange(lead)

    def lead_cols(inc_x, x_g, start):
        base = contract_rows(inc_x, inc_lead)
        slack_x = lax.dynamic_slice_in_dim(slack_ord, start, x_g.shape[0])
        diag = jnp.where(x_g[:, None] == lead_g[None, :], slack_x[:, None], 0.0)
        return base + diag

    a_lead = lead_cols(inc_lead, lead_g, 0)
    f0, f1 = 0, PANEL
    l0, inv0 = chol_inv(a_lead[f0:f1, f0:f1])
    b0 = solve_rows(a_lead[f1:, f0:f1], inv0)
    head0 = jnp.concatenate([l0, b0], 0)
    rb0 = b0.astype(jnp.bfloat16)
    a11 = a_lead[f1:, f1:] - lax.dot_general(
        rb0, rb0, (((1,), (1,)), ((), ())), preferred_element_type=jnp.float32
    )
    l1, inv1 = chol_inv(a11)
    head1 = jnp.concatenate([jnp.zeros_like(l1), l1], 0)

    m_rows = lead_cols(inc_rows, rows_g, link_idx * rows_dev)
    m_cols = lead_cols(inc_cols, cols_g, col_idx * cols_dev)

    def panels(m_x, at_top):
        col0 = head_fix(solve_rows(m_x[:, f0:f1], inv0), at_top, head0)
        r0 = col0.astype(jnp.bfloat16)
        m1 = m_x[:, f1:] - lax.dot_general(
            r0, rb0, (((1,), (1,)), ((), ())), preferred_element_type=jnp.float32
        )
        col1 = head_fix(solve_rows(m1, inv1), at_top, head1)
        return col0, col1

    col0_r, col1_r = panels(m_rows, link_idx == 0)
    col0_c, col1_c = panels(m_cols, col_idx == 0)
    left_t = jnp.concatenate(
        [inc_rows, col0_r.astype(jnp.bfloat16).T, col1_r.astype(jnp.bfloat16).T], 0
    )
    right_t = jnp.concatenate(
        [inc_cols, -col0_c.astype(jnp.bfloat16).T, -col1_c.astype(jnp.bfloat16).T], 0
    )
    matrix = contract_rows(left_t, right_t)
    slack_rows = lax.dynamic_slice_in_dim(slack_ord, link_idx * rows_dev, rows_dev)
    matrix = matrix + jnp.where(
        rows_g[:, None] == cols_g[None, :], slack_rows[:, None], jnp.float32(0.0)
    )
    panel_block = jnp.concatenate([col0_r, col1_r], 1)
    padded = jnp.pad(panel_block, ((0, 0), (0, cols_dev - lead)))
    return jnp.where(
        cols_g[None, :] < lead,
        padded,
        jnp.where(rows_g[:, None] < lead, jnp.float32(0.0), matrix),
    )


def solution(mesh):
    in_specs = (P("link", None, None), P("link", None), P("link"), P(), P())
    out_specs = P("link", "col")
    return jax.shard_map(local, mesh=mesh, in_specs=in_specs, out_specs=out_specs, check_vma=False)
```

```python
import jax
import jax.numpy as jnp
from jax import lax
from jax.sharding import PartitionSpec as P
from jax.experimental import pallas as pl
from jax.experimental.pallas import tpu as pltpu

PANEL = 128
SUB = 8
HI = lax.Precision.HIGHEST
BLK = 8


def _chol_inv_kernel(a_ref, l_ref, inv_ref, work, binv, lt_ref):
    n = a_ref.shape[0]
    work[...] = a_ref[...]
    rr = lax.broadcasted_iota(jnp.int32, (n, n), 0)
    cc = lax.broadcasted_iota(jnp.int32, (n, n), 1)
    binv[...] = jnp.where(rr == cc, 1.0, 0.0).astype(jnp.float32)
    lane = lax.broadcasted_iota(jnp.int32, (BLK, n), 1)
    sub = lax.broadcasted_iota(jnp.int32, (BLK, n), 0)
    subc = lax.broadcasted_iota(jnp.int32, (BLK, 1), 0)

    def block(b, carry):
        base = pl.multiple_of(b * BLK, BLK)
        slab = work[pl.ds(base, BLK), :]
        bslab = binv[pl.ds(base, BLK), :]
        out = jnp.zeros((BLK, n), jnp.float32)
        xout = jnp.zeros((BLK, n), jnp.float32)
        for i in range(BLK):
            col = base + i
            rowi = jnp.sum(jnp.where(sub == i, slab, 0.0), axis=0, keepdims=True)
            d = jnp.sum(jnp.where(lane[0:1] == col, rowi, 0.0), axis=1, keepdims=True)
            s = 1.0 / jnp.sqrt(d)
            lrow = jnp.where(lane[0:1] >= col, rowi * s, 0.0)
            out = jnp.where(sub == i, lrow, out)
            colv = jnp.sum(jnp.where(lane == col, slab, 0.0), axis=1, keepdims=True) * s
            slab = slab - colv * lrow
            xi = jnp.sum(jnp.where(sub == i, bslab, 0.0), axis=0, keepdims=True) * s
            xout = jnp.where(sub == i, xi, xout)
            bslab = bslab - jnp.where(subc > i, colv, 0.0) * xi
        lt_ref[pl.ds(base, BLK), :] = out
        inv_ref[pl.ds(base, BLK), :] = xout
        out_t = out.T
        work[...] = work[...] - jnp.dot(out_t, out, precision=HI, preferred_element_type=jnp.float32)
        binv[...] = binv[...] - jnp.dot(out_t, xout, precision=HI, preferred_element_type=jnp.float32)
        return carry

    lax.fori_loop(0, n // BLK, block, 0)
    l_ref[...] = lt_ref[...].T


def chol_inv(a):
    n = a.shape[0]
    lt, inv = pl.pallas_call(
        _chol_inv_kernel,
        out_shape=(jax.ShapeDtypeStruct((n, n), jnp.float32), jax.ShapeDtypeStruct((n, n), jnp.float32)),
        scratch_shapes=[pltpu.VMEM((n, n), jnp.float32)] * 3,
    )(a)
    return lt, inv


def densify(vals, ids, targets):
    groups, rows, tile_len = vals.shape
    tpc = rows // SUB
    nt = targets.shape[0]
    hits = (ids[:, None, :] == targets[None, :, None]).astype(jnp.bfloat16)
    own = (jnp.arange(SUB)[:, None] == jnp.arange(rows)[None, :] // tpc).astype(jnp.bfloat16)
    spread = (hits[:, :, None, :] * own[None, None, :, :]).reshape(groups, nt * SUB, rows)
    dense_out = lax.dot_general(
        spread, vals, (((2,), (1,)), ((0,), (0,))), preferred_element_type=jnp.float32,
    )
    dense_out = dense_out.astype(jnp.bfloat16).reshape(groups, nt, SUB, tile_len)
    return dense_out.transpose(0, 2, 1, 3).reshape(groups * SUB, nt * tile_len)


def gather_links(part, link_devs):
    cores = 2
    zs = 8
    xs = link_devs // (zs * cores)

    def shifted(block, move):
        pairs = [(src, move(src)) for src in range(link_devs)]
        return lax.ppermute(block, "link", pairs)

    def zmove(step):
        return lambda l: (l // (zs * cores)) * zs * cores + (((l // cores) % zs + step) % zs) * cores + l % cores

    def xmove(step):
        return lambda l: ((l // (zs * cores) + step) % xs) * zs * cores + l % (zs * cores)

    got = jnp.stack([part] + [shifted(part, zmove(s)) for s in range(1, zs)], 0)
    got = jnp.concatenate([got] + [shifted(got, xmove(s)) for s in range(1, xs)], 0)
    return jnp.concatenate([got, shifted(got, lambda l: l ^ 1)], 0)


def contract_rows(left_side, right_side):
    return lax.dot_general(
        left_side, right_side, (((0,), (0,)), ((), ())), preferred_element_type=jnp.float32
    )


def lower_inverse(lower):
    eye = jnp.eye(lower.shape[0], dtype=jnp.float32)
    return jax.scipy.linalg.solve_triangular(lower, eye, lower=True)


def solve_rows(block, inv_lower):
    return lax.dot_general(
        block, inv_lower, (((1,), (1,)), ((), ())), precision=HI,
        preferred_element_type=jnp.float32,
    )


def head_fix(solved, at_top, head):
    top = jnp.where(at_top, head, solved[: head.shape[0]])
    return jnp.concatenate([top, solved[head.shape[0]:]], 0)


def local(values, tiles, barrier, slack, order):
    xs, zs, cores = lax.axis_size("x"), lax.axis_size("z"), lax.axis_size("core")
    link_devs = xs * zs * cores
    col_devs = lax.axis_size("col")
    link_idx = (lax.axis_index("x") * zs + lax.axis_index("z")) * cores + lax.axis_index("core")
    col_idx = lax.axis_index("col")
    plane = ("x", "z")
    swap = [(0, 1), (1, 0)]
    link_count = slack.shape[0]
    rows_dev = link_count // link_devs
    cols_dev = link_count // col_devs
    per_dev, tpc, tile_len = values.shape
    ntiles = order.shape[0]
    lead = 2 * PANEL
    lead_tiles = lead // tile_len
    row_tiles = rows_dev // tile_len
    col_tiles = cols_dev // tile_len
    factor = link_count / (per_dev * link_devs * tpc * tile_len)
    scaled = (jnp.sqrt(barrier * factor)[:, None, None] * values.astype(jnp.float32)).astype(
        jnp.bfloat16
    )
    own_rows = scaled.reshape(per_dev * tpc, tile_len)
    groups = per_dev // SUB
    own_lead = densify(
        own_rows.reshape(groups, SUB * tpc, tile_len), tiles.reshape(groups, SUB * tpc),
        order[:lead_tiles],
    )
    own_ids = jnp.pad(tiles.astype(jnp.bfloat16), ((0, 0), (0, tile_len - tpc)))
    small = jnp.concatenate([own_lead, own_ids], 1)
    copies = jnp.broadcast_to(small[None], (xs * zs,) + small.shape)
    half = lax.all_to_all(copies, plane, 0, 0, tiled=True)
    small_all = jnp.concatenate([half, lax.ppermute(half, "core", swap)], 0)
    small_all = small_all.reshape(-1, lead + tile_len)
    inc_lead = small_all[:, :lead]
    mine = lax.all_gather(own_rows, plane, axis=0)
    everyone = jnp.concatenate([mine, lax.ppermute(mine, "core", swap)], 0)
    devs = everyone.shape[0]
    ids_all = small_all[:, lead : lead + tpc].astype(jnp.int32)
    ids_all = ids_all.reshape(devs * groups, SUB * tpc)
    vals_all = everyone.reshape(devs * groups, SUB * tpc, tile_len)

    inc_rows = densify(
        vals_all, ids_all, lax.dynamic_slice_in_dim(order, link_idx * row_tiles, row_tiles)
    )
    inc_cols = densify(
        vals_all, ids_all, lax.dynamic_slice_in_dim(order, col_idx * col_tiles, col_tiles)
    )

    slack_ord = jnp.take(slack.reshape(ntiles, tile_len), order, axis=0).reshape(link_count)
    rows_g = link_idx * rows_dev + jnp.arange(rows_dev)
    cols_g = col_idx * cols_dev + jnp.arange(cols_dev)
    lead_g = jnp.arange(lead)

    def lead_cols(inc_x, x_g, start):
        base = contract_rows(inc_x, inc_lead)
        slack_x = lax.dynamic_slice_in_dim(slack_ord, start, x_g.shape[0])
        diag = jnp.where(x_g[:, None] == lead_g[None, :], slack_x[:, None], 0.0)
        return base + diag

    a_lead = lead_cols(inc_lead, lead_g, 0)
    f0, f1 = 0, PANEL
    l0, inv0 = chol_inv(a_lead[f0:f1, f0:f1])
    b0 = solve_rows(a_lead[f1:, f0:f1], inv0)
    head0 = jnp.concatenate([l0, b0], 0)
    rb0 = b0.astype(jnp.bfloat16)
    a11 = a_lead[f1:, f1:] - lax.dot_general(
        rb0, rb0, (((1,), (1,)), ((), ())), preferred_element_type=jnp.float32
    )
    l1, inv1 = chol_inv(a11)
    head1 = jnp.concatenate([jnp.zeros_like(l1), l1], 0)

    m_rows = lead_cols(inc_rows, rows_g, link_idx * rows_dev)
    m_cols = lead_cols(inc_cols, cols_g, col_idx * cols_dev)

    def panels(m_x, at_top):
        col0 = head_fix(solve_rows(m_x[:, f0:f1], inv0), at_top, head0)
        r0 = col0.astype(jnp.bfloat16)
        m1 = m_x[:, f1:] - lax.dot_general(
            r0, rb0, (((1,), (1,)), ((), ())), preferred_element_type=jnp.float32
        )
        col1 = head_fix(solve_rows(m1, inv1), at_top, head1)
        return col0, col1

    col0_r, col1_r = panels(m_rows, link_idx == 0)
    col0_c, col1_c = panels(m_cols, col_idx == 0)
    left = jnp.concatenate(
        [inc_rows.T, col0_r.astype(jnp.bfloat16), col1_r.astype(jnp.bfloat16)], 1
    )
    right_t = jnp.concatenate(
        [inc_cols, -col0_c.astype(jnp.bfloat16).T, -col1_c.astype(jnp.bfloat16).T], 0
    )
    matrix = jnp.dot(left, right_t, preferred_element_type=jnp.float32)
    slack_rows = lax.dynamic_slice_in_dim(slack_ord, link_idx * rows_dev, rows_dev)
    matrix = matrix + jnp.where(
        rows_g[:, None] == cols_g[None, :], slack_rows[:, None], jnp.float32(0.0)
    )
    panel_block = jnp.concatenate([col0_r, col1_r], 1)
    padded = jnp.pad(panel_block, ((0, 0), (0, cols_dev - lead)))
    return jnp.where(
        cols_g[None, :] < lead,
        padded,
        jnp.where(rows_g[:, None] < lead, jnp.float32(0.0), matrix),
    )


def solution(mesh):
    links = ("x", "z", "core")
    col_devs = mesh.shape["col"]
    split = mesh.devices.reshape(-1, 8, 2, col_devs)
    fine = jax.sharding.Mesh(split, links + ("col",))
    in_specs = (P(links, None, None), P(links, None), P(links), P(), P())
    out_specs = P(links, "col")
    return jax.shard_map(local, mesh=fine, in_specs=in_specs, out_specs=out_specs, check_vma=False)
```

```python
import jax
import jax.numpy as jnp
from jax import lax
from jax.sharding import PartitionSpec as P
from jax.experimental import pallas as pl
from jax.experimental.pallas import tpu as pltpu

PANEL = 128
SUB = 8
HI = lax.Precision.HIGHEST
BLK = 8


def _chol_inv_kernel(a_ref, l_ref, inv_ref, work, binv, lt_ref):
    n = a_ref.shape[0]
    work[...] = a_ref[...]
    rr = lax.broadcasted_iota(jnp.int32, (n, n), 0)
    cc = lax.broadcasted_iota(jnp.int32, (n, n), 1)
    binv[...] = jnp.where(rr == cc, 1.0, 0.0).astype(jnp.float32)
    lane = lax.broadcasted_iota(jnp.int32, (BLK, n), 1)
    sub = lax.broadcasted_iota(jnp.int32, (BLK, n), 0)
    subc = lax.broadcasted_iota(jnp.int32, (BLK, 1), 0)

    def block(b, carry):
        base = pl.multiple_of(b * BLK, BLK)
        slab = work[pl.ds(base, BLK), :]
        bslab = binv[pl.ds(base, BLK), :]
        out = jnp.zeros((BLK, n), jnp.float32)
        xout = jnp.zeros((BLK, n), jnp.float32)
        for i in range(BLK):
            col = base + i
            rowi = jnp.sum(jnp.where(sub == i, slab, 0.0), axis=0, keepdims=True)
            d = jnp.sum(jnp.where(lane[0:1] == col, rowi, 0.0), axis=1, keepdims=True)
            s = 1.0 / jnp.sqrt(d)
            lrow = jnp.where(lane[0:1] >= col, rowi * s, 0.0)
            out = jnp.where(sub == i, lrow, out)
            colv = jnp.sum(jnp.where(lane == col, slab, 0.0), axis=1, keepdims=True) * s
            slab = slab - colv * lrow
            xi = jnp.sum(jnp.where(sub == i, bslab, 0.0), axis=0, keepdims=True) * s
            xout = jnp.where(sub == i, xi, xout)
            bslab = bslab - jnp.where(subc > i, colv, 0.0) * xi
        lt_ref[pl.ds(base, BLK), :] = out
        inv_ref[pl.ds(base, BLK), :] = xout
        out_t = out.T
        work[...] = work[...] - jnp.dot(out_t, out, precision=HI, preferred_element_type=jnp.float32)
        binv[...] = binv[...] - jnp.dot(out_t, xout, precision=HI, preferred_element_type=jnp.float32)
        return carry

    lax.fori_loop(0, n // BLK, block, 0)
    l_ref[...] = lt_ref[...].T


def chol_inv(a):
    n = a.shape[0]
    lt, inv = pl.pallas_call(
        _chol_inv_kernel,
        out_shape=(jax.ShapeDtypeStruct((n, n), jnp.float32), jax.ShapeDtypeStruct((n, n), jnp.float32)),
        scratch_shapes=[pltpu.VMEM((n, n), jnp.float32)] * 3,
    )(a)
    return lt, inv


def densify(vals, ids, targets):
    groups, rows, tile_len = vals.shape
    tpc = rows // SUB
    nt = targets.shape[0]
    hits = (ids[:, None, :] == targets[None, :, None]).astype(jnp.bfloat16)
    own = (jnp.arange(SUB)[:, None] == jnp.arange(rows)[None, :] // tpc).astype(jnp.bfloat16)
    spread = (hits[:, :, None, :] * own[None, None, :, :]).reshape(groups, nt * SUB, rows)
    dense_out = lax.dot_general(
        spread, vals, (((2,), (1,)), ((0,), (0,))), preferred_element_type=jnp.float32,
    )
    dense_out = dense_out.astype(jnp.bfloat16).reshape(groups, nt, SUB, tile_len)
    return dense_out.transpose(0, 2, 1, 3).reshape(groups * SUB, nt * tile_len)


def densify_narrow(vals, ids, targets):
    groups, rows, tile_len = vals.shape
    tpc = rows // SUB
    nt = targets.shape[0]
    hits = (ids[:, None, :] == targets[None, :, None]).astype(jnp.bfloat16)
    own = (jnp.arange(SUB)[:, None] == jnp.arange(rows)[None, :] // tpc).astype(jnp.bfloat16)
    spread = (hits[:, :, None, :] * own[None, None, :, :]).reshape(groups, nt * SUB, rows)
    dense_t = lax.dot_general(
        vals, spread, (((1,), (2,)), ((0,), (0,))), preferred_element_type=jnp.float32,
    )
    dense_t = dense_t.astype(jnp.bfloat16).reshape(groups, tile_len, nt, SUB)
    return dense_t.transpose(0, 3, 2, 1).reshape(groups * SUB, nt * tile_len)


def gather_links(part, link_devs):
    cores = 2
    zs = 8
    xs = link_devs // (zs * cores)

    def shifted(block, move):
        pairs = [(src, move(src)) for src in range(link_devs)]
        return lax.ppermute(block, "link", pairs)

    def zmove(step):
        return lambda l: (l // (zs * cores)) * zs * cores + (((l // cores) % zs + step) % zs) * cores + l % cores

    def xmove(step):
        return lambda l: ((l // (zs * cores) + step) % xs) * zs * cores + l % (zs * cores)

    got = jnp.stack([part] + [shifted(part, zmove(s)) for s in range(1, zs)], 0)
    got = jnp.concatenate([got] + [shifted(got, xmove(s)) for s in range(1, xs)], 0)
    return jnp.concatenate([got, shifted(got, lambda l: l ^ 1)], 0)


def contract_rows(left_side, right_side):
    return lax.dot_general(
        left_side, right_side, (((0,), (0,)), ((), ())), preferred_element_type=jnp.float32
    )


def lower_inverse(lower):
    eye = jnp.eye(lower.shape[0], dtype=jnp.float32)
    return jax.scipy.linalg.solve_triangular(lower, eye, lower=True)


def solve_rows(block, inv_lower, precision=HI):
    return lax.dot_general(
        block, inv_lower, (((1,), (1,)), ((), ())), precision=precision,
        preferred_element_type=jnp.float32,
    )


def head_fix(solved, at_top, head):
    top = jnp.where(at_top, head, solved[: head.shape[0]])
    return jnp.concatenate([top, solved[head.shape[0]:]], 0)


def local(values, tiles, barrier, slack, order):
    link_devs = lax.axis_size("link")
    col_devs = lax.axis_size("col")
    link_idx = lax.axis_index("link")
    col_idx = lax.axis_index("col")
    link_count = slack.shape[0]
    rows_dev = link_count // link_devs
    cols_dev = link_count // col_devs
    per_dev, tpc, tile_len = values.shape
    ntiles = order.shape[0]
    lead = 2 * PANEL
    lead_tiles = lead // tile_len
    row_tiles = rows_dev // tile_len
    col_tiles = cols_dev // tile_len
    factor = link_count / (per_dev * link_devs * tpc * tile_len)
    scaled = (jnp.sqrt(barrier * factor)[:, None, None] * values.astype(jnp.float32)).astype(
        jnp.bfloat16
    )
    own_rows = scaled.reshape(per_dev * tpc, tile_len)
    groups = per_dev // SUB
    own_lead = densify(
        own_rows.reshape(groups, SUB * tpc, tile_len), tiles.reshape(groups, SUB * tpc),
        order[:lead_tiles],
    )
    own_ids = jnp.pad(tiles.astype(jnp.bfloat16), ((0, 0), (0, tile_len - tpc)))
    small = jnp.concatenate([own_lead, own_ids], 1)
    copies = jnp.broadcast_to(small[None], (link_devs,) + small.shape)
    small_all = lax.all_to_all(copies, "link", 0, 0, tiled=True).reshape(-1, lead + tile_len)
    inc_lead = small_all[:, :lead]
    everyone = lax.all_gather(own_rows, "link", axis=0)
    devs = everyone.shape[0]
    ids_all = small_all[:, lead : lead + tpc].astype(jnp.int32)
    ids_all = ids_all.reshape(devs * groups, SUB * tpc)
    vals_all = everyone.reshape(devs * groups, SUB * tpc, tile_len)

    inc_rows = densify_narrow(
        vals_all, ids_all, lax.dynamic_slice_in_dim(order, link_idx * row_tiles, row_tiles)
    )
    inc_cols = densify(
        vals_all, ids_all, lax.dynamic_slice_in_dim(order, col_idx * col_tiles, col_tiles)
    )

    slack_ord = jnp.take(slack.reshape(ntiles, tile_len), order, axis=0).reshape(link_count)
    rows_g = link_idx * rows_dev + jnp.arange(rows_dev)
    cols_g = col_idx * cols_dev + jnp.arange(cols_dev)
    lead_g = jnp.arange(lead)

    def lead_cols(inc_x, x_g, start):
        base = contract_rows(inc_x, inc_lead)
        slack_x = lax.dynamic_slice_in_dim(slack_ord, start, x_g.shape[0])
        diag = jnp.where(x_g[:, None] == lead_g[None, :], slack_x[:, None], 0.0)
        return base + diag

    a_lead = lead_cols(inc_lead, lead_g, 0)
    f0, f1 = 0, PANEL
    l0, inv0 = chol_inv(a_lead[f0:f1, f0:f1])
    b0 = solve_rows(a_lead[f1:, f0:f1], inv0)
    head0 = jnp.concatenate([l0, b0], 0)
    rb0 = b0.astype(jnp.bfloat16)
    a11 = a_lead[f1:, f1:] - lax.dot_general(
        rb0, rb0, (((1,), (1,)), ((), ())), preferred_element_type=jnp.float32
    )
    l1, inv1 = chol_inv(a11)
    head1 = jnp.concatenate([jnp.zeros_like(l1), l1], 0)

    m_rows = lead_cols(inc_rows, rows_g, link_idx * rows_dev)
    m_cols = lead_cols(inc_cols, cols_g, col_idx * cols_dev)

    def panels(m_x, at_top):
        col0 = head_fix(solve_rows(m_x[:, f0:f1], inv0, lax.Precision.HIGH), at_top, head0)
        r0 = col0.astype(jnp.bfloat16)
        m1 = m_x[:, f1:] - lax.dot_general(
            r0, rb0, (((1,), (1,)), ((), ())), preferred_element_type=jnp.float32
        )
        col1 = head_fix(solve_rows(m1, inv1, lax.Precision.HIGH), at_top, head1)
        return col0, col1

    col0_r, col1_r = panels(m_rows, link_idx == 0)
    col0_c, col1_c = panels(m_cols, col_idx == 0)
    left = jnp.concatenate(
        [inc_rows.T, col0_r.astype(jnp.bfloat16), col1_r.astype(jnp.bfloat16)], 1
    )
    right_t = jnp.concatenate(
        [inc_cols, -col0_c.astype(jnp.bfloat16).T, -col1_c.astype(jnp.bfloat16).T], 0
    )
    matrix = jnp.dot(left, right_t, preferred_element_type=jnp.float32)
    slack_rows = lax.dynamic_slice_in_dim(slack_ord, link_idx * rows_dev, rows_dev)
    matrix = matrix + jnp.where(
        rows_g[:, None] == cols_g[None, :], slack_rows[:, None], jnp.float32(0.0)
    )
    panel_block = jnp.concatenate([col0_r, col1_r], 1)
    padded = jnp.pad(panel_block, ((0, 0), (0, cols_dev - lead)))
    return jnp.where(
        cols_g[None, :] < lead,
        padded,
        jnp.where(rows_g[:, None] < lead, jnp.float32(0.0), matrix),
    )


def solution(mesh):
    in_specs = (P("link", None, None), P("link", None), P("link"), P(), P())
    out_specs = P("link", "col")
    return jax.shard_map(local, mesh=mesh, in_specs=in_specs, out_specs=out_specs, check_vma=False)
```

```python
import jax
import jax.numpy as jnp
from jax import lax
from jax.sharding import PartitionSpec as P
from jax.experimental import pallas as pl
from jax.experimental.pallas import tpu as pltpu

PANEL = 128
SUB = 8
HI = lax.Precision.HIGHEST
BLK = 8


def _chol_inv_kernel(a_ref, l_ref, inv_ref, work, binv, lt_ref):
    n = a_ref.shape[0]
    work[...] = a_ref[...]
    rr = lax.broadcasted_iota(jnp.int32, (n, n), 0)
    cc = lax.broadcasted_iota(jnp.int32, (n, n), 1)
    binv[...] = jnp.where(rr == cc, 1.0, 0.0).astype(jnp.float32)
    lane = lax.broadcasted_iota(jnp.int32, (BLK, n), 1)
    sub = lax.broadcasted_iota(jnp.int32, (BLK, n), 0)
    subc = lax.broadcasted_iota(jnp.int32, (BLK, 1), 0)

    def block(b, carry):
        base = pl.multiple_of(b * BLK, BLK)
        slab = work[pl.ds(base, BLK), :]
        bslab = binv[pl.ds(base, BLK), :]
        out = jnp.zeros((BLK, n), jnp.float32)
        xout = jnp.zeros((BLK, n), jnp.float32)
        for i in range(BLK):
            col = base + i
            rowi = jnp.sum(jnp.where(sub == i, slab, 0.0), axis=0, keepdims=True)
            d = jnp.sum(jnp.where(lane[0:1] == col, rowi, 0.0), axis=1, keepdims=True)
            s = 1.0 / jnp.sqrt(d)
            lrow = jnp.where(lane[0:1] >= col, rowi * s, 0.0)
            out = jnp.where(sub == i, lrow, out)
            colv = jnp.sum(jnp.where(lane == col, slab, 0.0), axis=1, keepdims=True) * s
            slab = slab - colv * lrow
            xi = jnp.sum(jnp.where(sub == i, bslab, 0.0), axis=0, keepdims=True) * s
            xout = jnp.where(sub == i, xi, xout)
            bslab = bslab - jnp.where(subc > i, colv, 0.0) * xi
        lt_ref[pl.ds(base, BLK), :] = out
        inv_ref[pl.ds(base, BLK), :] = xout
        out_t = out.T
        work[...] = work[...] - jnp.dot(out_t, out, precision=HI, preferred_element_type=jnp.float32)
        binv[...] = binv[...] - jnp.dot(out_t, xout, precision=HI, preferred_element_type=jnp.float32)
        return carry

    lax.fori_loop(0, n // BLK, block, 0)
    l_ref[...] = lt_ref[...].T


def chol_inv(a):
    n = a.shape[0]
    lt, inv = pl.pallas_call(
        _chol_inv_kernel,
        out_shape=(jax.ShapeDtypeStruct((n, n), jnp.float32), jax.ShapeDtypeStruct((n, n), jnp.float32)),
        scratch_shapes=[pltpu.VMEM((n, n), jnp.float32)] * 3,
    )(a)
    return lt, inv


def densify(vals, ids, targets):
    groups, rows, tile_len = vals.shape
    tpc = rows // SUB
    nt = targets.shape[0]
    hits = (ids[:, None, :] == targets[None, :, None]).astype(jnp.bfloat16)
    own = (jnp.arange(SUB)[:, None] == jnp.arange(rows)[None, :] // tpc).astype(jnp.bfloat16)
    spread = (hits[:, :, None, :] * own[None, None, :, :]).reshape(groups, nt * SUB, rows)
    dense_out = lax.dot_general(
        spread, vals, (((2,), (1,)), ((0,), (0,))), preferred_element_type=jnp.float32,
    )
    dense_out = dense_out.astype(jnp.bfloat16).reshape(groups, nt, SUB, tile_len)
    return dense_out.transpose(0, 2, 1, 3).reshape(groups * SUB, nt * tile_len)


def gather_links(part, link_devs):
    cores = 2
    zs = 8
    xs = link_devs // (zs * cores)

    def shifted(block, move):
        pairs = [(src, move(src)) for src in range(link_devs)]
        return lax.ppermute(block, "link", pairs)

    def zmove(step):
        return lambda l: (l // (zs * cores)) * zs * cores + (((l // cores) % zs + step) % zs) * cores + l % cores

    def xmove(step):
        return lambda l: ((l // (zs * cores) + step) % xs) * zs * cores + l % (zs * cores)

    got = jnp.stack([part] + [shifted(part, zmove(s)) for s in range(1, zs)], 0)
    got = jnp.concatenate([got] + [shifted(got, xmove(s)) for s in range(1, xs)], 0)
    return jnp.concatenate([got, shifted(got, lambda l: l ^ 1)], 0)


def contract_rows(left_side, right_side):
    return lax.dot_general(
        left_side, right_side, (((0,), (0,)), ((), ())), preferred_element_type=jnp.float32
    )


def lower_inverse(lower):
    eye = jnp.eye(lower.shape[0], dtype=jnp.float32)
    return jax.scipy.linalg.solve_triangular(lower, eye, lower=True)


def solve_rows(block, inv_lower, precision=HI):
    return lax.dot_general(
        block, inv_lower, (((1,), (1,)), ((), ())), precision=precision,
        preferred_element_type=jnp.float32,
    )


def head_fix(solved, at_top, head):
    top = jnp.where(at_top, head, solved[: head.shape[0]])
    return jnp.concatenate([top, solved[head.shape[0]:]], 0)


def local(values, tiles, barrier, slack, order):
    link_devs = lax.axis_size("link")
    col_devs = lax.axis_size("col")
    link_idx = lax.axis_index("link")
    col_idx = lax.axis_index("col")
    link_count = slack.shape[0]
    rows_dev = link_count // link_devs
    cols_dev = link_count // col_devs
    per_dev, tpc, tile_len = values.shape
    ntiles = order.shape[0]
    lead = 2 * PANEL
    lead_tiles = lead // tile_len
    row_tiles = rows_dev // tile_len
    col_tiles = cols_dev // tile_len
    factor = link_count / (per_dev * link_devs * tpc * tile_len)
    scaled = (jnp.sqrt(barrier * factor)[:, None, None] * values.astype(jnp.float32)).astype(
        jnp.bfloat16
    )
    own_rows = scaled.reshape(per_dev * tpc, tile_len)
    groups = per_dev // SUB
    own_lead = densify(
        own_rows.reshape(groups, SUB * tpc, tile_len), tiles.reshape(groups, SUB * tpc),
        order[:lead_tiles],
    )
    own_ids = jnp.pad(tiles.astype(jnp.bfloat16), ((0, 0), (0, tile_len - tpc)))
    small = jnp.concatenate([own_lead, own_ids], 1)
    copies = jnp.broadcast_to(small[None], (link_devs,) + small.shape)
    small_all = lax.all_to_all(copies, "link", 0, 0, tiled=True).reshape(-1, lead + tile_len)
    inc_lead = small_all[:, :lead]
    everyone = lax.all_gather(own_rows, "link", axis=0)
    devs = everyone.shape[0]
    ids_all = small_all[:, lead : lead + tpc].astype(jnp.int32)
    ids_all = ids_all.reshape(devs * groups, SUB * tpc)
    vals_all = everyone.reshape(devs * groups, SUB * tpc, tile_len)

    inc_rows = densify(
        vals_all, ids_all, lax.dynamic_slice_in_dim(order, link_idx * row_tiles, row_tiles)
    )
    inc_cols = densify(
        vals_all, ids_all, lax.dynamic_slice_in_dim(order, col_idx * col_tiles, col_tiles)
    )

    slack_ord = jnp.take(slack.reshape(ntiles, tile_len), order, axis=0).reshape(link_count)
    rows_g = link_idx * rows_dev + jnp.arange(rows_dev)
    cols_g = col_idx * cols_dev + jnp.arange(cols_dev)
    lead_g = jnp.arange(lead)

    def lead_cols(inc_x, x_g, start):
        base = contract_rows(inc_x, inc_lead)
        slack_x = lax.dynamic_slice_in_dim(slack_ord, start, x_g.shape[0])
        diag = jnp.where(x_g[:, None] == lead_g[None, :], slack_x[:, None], 0.0)
        return base + diag

    a_lead = lead_cols(inc_lead, lead_g, 0)
    f0, f1 = 0, PANEL
    l0, inv0 = chol_inv(a_lead[f0:f1, f0:f1])
    b0 = solve_rows(a_lead[f1:, f0:f1], inv0)
    head0 = jnp.concatenate([l0, b0], 0)
    rb0 = b0.astype(jnp.bfloat16)
    a11 = a_lead[f1:, f1:] - lax.dot_general(
        rb0, rb0, (((1,), (1,)), ((), ())), preferred_element_type=jnp.float32
    )
    l1, inv1 = chol_inv(a11)
    head1 = jnp.concatenate([jnp.zeros_like(l1), l1], 0)

    m_rows = lead_cols(inc_rows, rows_g, link_idx * rows_dev)
    slack_c = lax.dynamic_slice_in_dim(slack_ord, col_idx * cols_dev, cols_dev)
    m_t = contract_rows(inc_lead, inc_cols) + jnp.where(
        lead_g[:, None] == cols_g[None, :], slack_c[None, :], 0.0
    )

    def panels(m_x, at_top):
        col0 = head_fix(solve_rows(m_x[:, f0:f1], inv0, lax.Precision.HIGH), at_top, head0)
        r0 = col0.astype(jnp.bfloat16)
        m1 = m_x[:, f1:] - lax.dot_general(
            r0, rb0, (((1,), (1,)), ((), ())), preferred_element_type=jnp.float32
        )
        col1 = head_fix(solve_rows(m1, inv1, lax.Precision.HIGH), at_top, head1)
        return col0, col1

    col0_r, col1_r = panels(m_rows, link_idx == 0)
    c_top = col_idx == 0

    def left_solve(inv_lower, block):
        return jnp.dot(inv_lower, block, precision=lax.Precision.HIGH,
                       preferred_element_type=jnp.float32)

    def col_fix(solved_t, head):
        top = jnp.where(c_top, head.T, solved_t[:, : head.shape[0]])
        return jnp.concatenate([top, solved_t[:, head.shape[0]:]], 1)

    c0t = col_fix(left_solve(inv0, m_t[f0:f1]), head0)
    r0t = c0t.astype(jnp.bfloat16)
    m1t = m_t[f1:] - jnp.dot(rb0, r0t, preferred_element_type=jnp.float32)
    c1t = col_fix(left_solve(inv1, m1t), head1)
    left = jnp.concatenate(
        [inc_rows.T, col0_r.astype(jnp.bfloat16), col1_r.astype(jnp.bfloat16)], 1
    )
    right_t = jnp.concatenate(
        [inc_cols, -r0t, -c1t.astype(jnp.bfloat16)], 0
    )
    matrix = jnp.dot(left, right_t, preferred_element_type=jnp.float32)
    slack_rows = lax.dynamic_slice_in_dim(slack_ord, link_idx * rows_dev, rows_dev)
    matrix = matrix + jnp.where(
        rows_g[:, None] == cols_g[None, :], slack_rows[:, None], jnp.float32(0.0)
    )
    panel_block = jnp.concatenate([col0_r, col1_r], 1)
    padded = jnp.pad(panel_block, ((0, 0), (0, cols_dev - lead)))
    return jnp.where(
        cols_g[None, :] < lead,
        padded,
        jnp.where(rows_g[:, None] < lead, jnp.float32(0.0), matrix),
    )


def solution(mesh):
    in_specs = (P("link", None, None), P("link", None), P("link"), P(), P())
    out_specs = P("link", "col")
    return jax.shard_map(local, mesh=mesh, in_specs=in_specs, out_specs=out_specs, check_vma=False)
```
